512 devices in a mesh: dp: 8 (over y, core), expert: 64 (over z, x).
Axes of the slice: x: 4, y: 4, z: 16, core: 2. Of those that a mesh axis runs over, the one named last changes fastest.
Arguments:
- out_grad: bfloat16 [65536, 3584], P(('dp', 'expert')), may hold values from -6 to 6
- gate_probs: bfloat16 [65536, 1], P(('dp', 'expert')), may hold values from 0.049804688 to 1
- copy_ids: int32 [65536, 1], P(('dp', 'expert')), may hold values from 0 to 63; in each aligned block of 128 rows (0 to 127, 128 to 255, ...) at most 3 rows name the same one
- copy_expert: int32 [64], replicated, may hold values from 0 to 47, as said below
- w_down: bfloat16 [64, 1024, 3584], P('expert', 'dp'), may hold values from -0.09375 to 0.09375
- swiglu_in: bfloat16 [64, 2, 1536, 1024], P('expert', None, None, 'dp'), may hold values from -6 to 6
Outputs:
- grad_swiglu_in: bfloat16 [64, 2, 1536, 1024], P('expert', None, None, 'dp')
- grad_w_down: bfloat16 [64, 1024, 3584], P('expert', 'dp')
- grad_gate_probs: float32 [65536, 1], P(('dp', 'expert'))
The draws below stay inside these ranges and needn't reach their ends.
Inputs may be any that keep to these rules, and one draw needn't show every extreme that they name: `copy_ids`: the rows of one device name one copy at most 3 times. `copy_expert`: each of the 48 experts is held by one or two copies; 16 experts are held by two.
All inputs are finite; a program needn't handle non-finite values.
Results may differ from the reference program's by a relative error of at most 0.0063.
Values may be sent and summed in bfloat16 or wider, within the bound.
No kernel may reach another device: no remote copies, remote signals or barrier semaphores. Data moves between devices by JAX's collectives and lax.ppermute only.
A program may use at most 128 MiB of HBM per device.

```python
import math
import jax
import jax.numpy as jnp
import numpy as np
from jax import lax

D = 3584
H = 1024
TOP = 1
TOK_DEV = 128
SLOT = 3
COPIES = 64
REDUNDANT = 16
EXPERTS = 48
TOKENS = 65536
ROWS_COL = 1536
DEVICES = 512


def draw_copy_expert(key, part):
    first_key = jax.random.fold_in(key, 11)
    second_key = jax.random.fold_in(key, 23)
    extra = jax.random.permutation(first_key, EXPERTS)[:REDUNDANT]
    table = jnp.concatenate([jnp.arange(EXPERTS, dtype=jnp.int32), extra.astype(jnp.int32)])
    return jax.random.permutation(second_key, table).astype(jnp.int32)


def block_scale(rng, extent, pieces, low, largest):
    factor_of = 1.0
    for dim, parts in pieces:
        draws = jax.random.uniform(jax.random.fold_in(jax.random.fold_in(rng, 6), dim), (parts,), jnp.float32, low / len(pieces), largest / len(pieces))
        factor_of = factor_of * jnp.repeat(jnp.exp(draws), extent[dim] // parts).reshape((-1,) + (1,) * (len(extent) - 1 - dim))
    return factor_of


def shared_out(key, own, number, rows, amount, top, reach, slope):
    sequence = jax.random.permutation(key, amount)
    crowded, usual = load_shares(amount, rows * top, reach, slope, True), load_shares(amount, rows * top, reach, slope, False)
    places = jnp.arange(amount)

    def named(tallies, rotation):
        used = int((tallies > 0).sum())
        fixed = max(1, used // 4)
        shifted = fixed + (places - fixed + rotation * (used - fixed)) % max(1, amount - fixed)
        return jnp.zeros((amount,), jnp.int32).at[sequence[jnp.where(places < fixed, places, shifted)]].set(jnp.asarray(tallies, jnp.int32))

    tallies = jnp.where(number % 4 == 0, named(crowded, number // 4), named(usual, number - number // 4 - 1))
    mixed = jax.random.permutation(jax.random.fold_in(own, 3), amount)
    giver, receiver = mixed[0:amount // 2 * 2:2], mixed[1:amount // 2 * 2:2]
    room = jnp.minimum(tallies[giver] - 1, reach - tallies[receiver]) // 2
    room = jnp.where((giver == sequence[0]) | (receiver == sequence[0]) | (tallies[receiver] == 0), 0, jnp.maximum(room, 0))
    shifted = jax.random.randint(jax.random.fold_in(own, 4), (amount // 2,), 0, 1 << 20) % (room + 1)
    tallies = tallies.at[giver].add(-shifted).at[receiver].add(shifted)
    items = jnp.searchsorted(jnp.cumsum(tallies), jnp.arange(rows * top), side="right").astype(jnp.int32)
    grid = items.reshape(top, rows).T
    grid = grid[jax.random.permutation(jax.random.fold_in(own, 1), rows)]
    rotation = jax.random.randint(jax.random.fold_in(own, 2), (rows, 1), 0, top)
    return jnp.take_along_axis(grid, (jnp.arange(top)[None, :] + rotation) % top, axis=1)


def load_shares(count, total, reach, slope, full):
    portions = [(1 << 20) // math.isqrt(grade ** slope) + 1 for grade in range(1, count + 1)]
    largest = reach if full else min(reach, max(-(-total // count), total * portions[0] // sum(portions)))
    least = 1 if total - largest >= count - 1 else 0
    counts, spare = [largest] + [least] * (count - 1), total - largest - least * (count - 1)
    while spare > 0:
        free = [i for i in range(1, count) if counts[i] < largest] or [i for i in range(1, count) if counts[i] < reach]
        pool, left = sum([portions[i] for i in free]), spare
        for i in free:
            more = min(reach - counts[i], max(1, left * portions[i] // pool), spare)
            counts[i] = counts[i] + more
            spare = spare - more
    return np.array(counts)


def noise(rng, extent, deviation, limit, cuts=(), kind=jnp.bfloat16):
    drawn = jax.random.normal(rng, extent, jnp.float32) * deviation
    if len(cuts) > 0:
        drawn = block_scale(rng, extent, cuts, -0.22, 0.18) * drawn
    return jnp.clip(drawn, min=-limit, max=limit).astype(kind)


def setup_inputs(seed: int = 0) -> dict:
    key_list = jax.random.split(jax.random.key(seed), 7)
    out_grad = noise(key_list[0], (TOKENS, D), 1.0, 6.0, ((0, 512),))
    gate_probs = jnp.clip(jnp.exp(math.log(1.0) - 2.9996462 * jax.random.uniform(key_list[1], (TOKENS, TOP), jnp.float32) ** block_scale(key_list[1], (TOKENS, TOP), ((0, 512),), -0.2, 0.2)), 0.049804688, 1.0).astype(jnp.bfloat16)
    copy_ids_keys = jax.random.split(jax.random.fold_in(key_list[2], 1), TOKENS // TOK_DEV)
    copy_ids_turns = jax.random.permutation(jax.random.fold_in(key_list[2], 3), TOKENS // TOK_DEV)
    copy_ids = jax.vmap(lambda own, number: shared_out(jax.random.fold_in(key_list[2], 2), own, number, TOK_DEV, COPIES, TOP, SLOT, 2))(copy_ids_keys, copy_ids_turns).reshape((TOKENS, TOP))
    copy_expert = draw_copy_expert(jax.random.fold_in(key_list[6], 71), 0)
    w_down = noise(key_list[4], (COPIES, H, D), D ** -0.5, 0.09375, ((0, 64), (1, 8)))
    swiglu_in = noise(key_list[5], (COPIES, 2, ROWS_COL, H), 1.0, 6.0, ((0, 64), (3, 8)))
    return {"out_grad": out_grad, "gate_probs": gate_probs, "copy_ids": copy_ids, "copy_expert": copy_expert, "w_down": w_down, "swiglu_in": swiglu_in}


def expert_work(rows, cache, weight):
    gate_pre = cache[0].astype(jnp.float32)
    up_pre = cache[1].astype(jnp.float32)
    sigmoid_gate = jax.nn.sigmoid(gate_pre)
    silu_gate = gate_pre * sigmoid_gate
    hidden = (silu_gate * up_pre).astype(jnp.bfloat16)
    grad_hidden = jnp.dot(rows, weight.T, preferred_element_type=jnp.float32)
    scores = jnp.sum(hidden.astype(jnp.float32) * grad_hidden, axis=1)
    grad_gate = grad_hidden * up_pre * sigmoid_gate * (1.0 + gate_pre * (1.0 - sigmoid_gate))
    grad_up = grad_hidden * silu_gate
    grad_cache = jnp.stack([grad_gate, grad_up]).astype(jnp.bfloat16)
    weight_grad = jnp.dot(hidden.T, rows, preferred_element_type=jnp.float32)
    return grad_cache, scores, weight_grad


def rank_block(block_ids):
    count_all = block_ids.shape[0]
    row_index = lax.broadcasted_iota(jnp.int32, (count_all, count_all), 0)
    col_index = lax.broadcasted_iota(jnp.int32, (count_all, count_all), 1)
    before = jnp.logical_and(block_ids[:, None] == block_ids[None, :], col_index < row_index)
    return jnp.sum(before.astype(jnp.int32), axis=1).astype(jnp.int32)


def reference(out_grad, gate_probs, copy_ids, copy_expert, w_down, swiglu_in):
    assigned = TOKENS * TOP
    per_device = TOK_DEV * TOP
    slot_rank = jax.vmap(rank_block)(copy_ids.reshape(DEVICES, per_device).astype(jnp.int32))
    device_of = (jnp.arange(assigned, dtype=jnp.int32) // per_device).astype(jnp.int32)
    target_row = (device_of * SLOT + slot_rank.reshape(assigned)).astype(jnp.int32)
    flat_copy = copy_ids.reshape(assigned).astype(jnp.int32)
    table = jnp.full((COPIES, ROWS_COL), -1, jnp.int32)
    table = table.at[flat_copy, target_row].set(jnp.arange(assigned, dtype=jnp.int32))
    flat_prob = gate_probs.reshape(assigned).astype(jnp.float32)

    def one_copy(inputs):
        weight, cache, index_row = inputs
        valid = index_row >= 0
        safe_index = jnp.where(valid, index_row, 0).astype(jnp.int32)
        token_index = (safe_index // TOP).astype(jnp.int32)
        values = flat_prob[safe_index][:, None] * out_grad[token_index].astype(jnp.float32)
        rows = jnp.where(valid[:, None], values, jnp.float32(0.0)).astype(jnp.bfloat16)
        grad_cache, scores, weight_grad = expert_work(rows, cache, weight)
        return grad_cache, scores, weight_grad.astype(jnp.bfloat16)

    grad_swiglu_in, scores, copy_grad = lax.map(one_copy, (w_down, swiglu_in, table))
    same_expert = (copy_expert[:, None] == copy_expert[None, :]).astype(jnp.float32)
    copy_wide = copy_grad.astype(jnp.float32)

    def join_copy(mask_row):
        summed = jnp.einsum("b,bhd->hd", mask_row, copy_wide, precision=lax.Precision.HIGHEST)
        return summed.astype(jnp.bfloat16)

    grad_w_down = lax.map(join_copy, same_expert)
    assigned_score = scores[flat_copy, target_row]
    grad_gate_probs = (assigned_score / flat_prob).reshape(TOKENS, TOP)
    return grad_swiglu_in, grad_w_down, grad_gate_probs
```

```python
import jax
import jax.numpy as jnp
from jax import lax
from jax.sharding import PartitionSpec as P

CHUNKS = 4


def activations(cache):
    gate_pre = cache[0].astype(jnp.float32)
    up_pre = cache[1].astype(jnp.float32)
    sigmoid_gate = jax.nn.sigmoid(gate_pre)
    silu_gate = gate_pre * sigmoid_gate
    hidden = (silu_gate * up_pre).astype(jnp.bfloat16)
    return (hidden, gate_pre, up_pre, sigmoid_gate, silu_gate)


def finish(grad_hidden, parts):
    hidden, gate_pre, up_pre, sigmoid_gate, silu_gate = parts
    scores = jnp.sum(hidden.astype(jnp.float32) * grad_hidden, axis=1)
    grad_gate = grad_hidden * up_pre * sigmoid_gate * (1.0 + gate_pre * (1.0 - sigmoid_gate))
    grad_up = grad_hidden * silu_gate
    grad_cache = jnp.stack([grad_gate, grad_up]).astype(jnp.bfloat16)
    return (grad_cache, scores)


def placement(flat_ids, slots, places):
    count_all = flat_ids.shape[0]
    row_index = lax.broadcasted_iota(jnp.int32, (count_all, count_all), 0)
    col_index = lax.broadcasted_iota(jnp.int32, (count_all, count_all), 1)
    before = jnp.logical_and(flat_ids[:, None] == flat_ids[None, :], col_index < row_index)
    slot_rank = jnp.sum(before.astype(jnp.int32), axis=1)
    target = flat_ids * slots + slot_rank
    return lax.broadcasted_iota(jnp.int32, (places, count_all), 0) == target[None, :]


def on_device(out_grad, gate_probs, copy_ids, copy_expert, w_down, swiglu_in):
    n_data = lax.axis_size("dp")
    n_expert = lax.axis_size("expert")
    cache = swiglu_in[0]
    weight = w_down[0]
    rows_all = cache.shape[1]
    hidden_dev = cache.shape[2]
    slots = rows_all // (n_data * n_expert)
    places = n_expert * slots
    width = out_grad.shape[1]
    tok_dev = out_grad.shape[0]
    top_count = copy_ids.shape[1]
    pair_count = tok_dev * top_count
    weighted = gate_probs.astype(jnp.float32)[:, :, None] * out_grad.astype(jnp.float32)[:, None, :]
    weighted = weighted.reshape(pair_count, width).astype(jnp.bfloat16)
    placing = placement(copy_ids.reshape(pair_count), slots, places)
    outgoing = jnp.dot(
        placing.astype(jnp.bfloat16), weighted, preferred_element_type=jnp.float32
    ).astype(jnp.bfloat16)
    outgoing = outgoing.reshape(n_expert, slots, width)
    parts = activations(cache)
    hidden = parts[0]
    chunk = width // CHUNKS
    grad_hidden = None
    col_parts = []
    for k in range(CHUNKS):
        send = outgoing[:, :, k * chunk:(k + 1) * chunk]
        arrived = lax.all_to_all(send, "expert", split_axis=0, concat_axis=0, tiled=True)
        rows_part = arrived.reshape(places, chunk)
        piece = lax.all_gather(rows_part, "dp", axis=0, tiled=True)
        part = lax.dot_general(
            piece, weight[:, k * chunk:(k + 1) * chunk], (((1,), (1,)), ((), ())),
            preferred_element_type=jnp.float32,
        )
        grad_hidden = part if grad_hidden is None else grad_hidden + part
        columns = lax.dot_general(
            hidden, piece, (((0,), (0,)), ((), ())), preferred_element_type=jnp.float32
        )
        col_parts.append(columns.astype(jnp.bfloat16))
    grad_cache, scores = finish(grad_hidden, parts)
    partial_scores = scores.reshape(n_data, n_expert, slots)
    returned = lax.all_to_all(
        lax.all_to_all(partial_scores, "dp", split_axis=0, concat_axis=0, tiled=True),
        "expert",
        split_axis=1,
        concat_axis=1,
        tiled=True,
    )
    score_back = jnp.sum(returned, axis=0).reshape(places)
    assigned_score = jnp.dot(
        placing.astype(jnp.float32).T, score_back, precision=lax.Precision.HIGHEST
    )
    grad_probs = (assigned_score / gate_probs.reshape(-1).astype(jnp.float32)).reshape(
        gate_probs.shape
    )
    copy_grad = jnp.concatenate(col_parts, axis=1)
    same_expert = (copy_expert[:, None] == copy_expert[None, :]).astype(jnp.float32)
    feature_blocks = copy_grad.reshape(hidden_dev, n_expert, width // n_expert)
    summed = jnp.einsum(
        "ab,nbd->nad",
        same_expert,
        lax.all_to_all(feature_blocks, "expert", split_axis=1, concat_axis=1, tiled=True).astype(
            jnp.float32
        ),
        precision=lax.Precision.HIGHEST,
    )
    joined = lax.all_to_all(
        summed.astype(jnp.bfloat16), "expert", split_axis=1, concat_axis=1, tiled=True
    )
    grad_weight = joined.reshape(1, hidden_dev, width)
    return (grad_cache[None], grad_weight, grad_probs)


def solution(mesh):
    placed = (
        P(("dp", "expert"), None),
        P(("dp", "expert"), None),
        P(("dp", "expert"), None),
        P(),
        P("expert", "dp", None),
        P("expert", None, None, "dp"),
    )
    return jax.shard_map(
        on_device,
        mesh=mesh,
        in_specs=placed,
        out_specs=(
            P("expert", None, None, "dp"),
            P("expert", "dp", None),
            P(("dp", "expert"), None),
        ),
        check_vma=False,
    )
```

```python
import jax
import jax.numpy as jnp
from jax import lax
from jax.sharding import PartitionSpec as P

CHUNKS = 1


def activations(cache):
    gate_pre = cache[0].astype(jnp.float32)
    up_pre = cache[1].astype(jnp.float32)
    sigmoid_gate = jax.nn.sigmoid(gate_pre)
    silu_gate = gate_pre * sigmoid_gate
    hidden = (silu_gate * up_pre).astype(jnp.bfloat16)
    return (hidden, gate_pre, up_pre, sigmoid_gate, silu_gate)


def finish(grad_hidden, parts):
    hidden, gate_pre, up_pre, sigmoid_gate, silu_gate = parts
    scores = jnp.sum(hidden.astype(jnp.float32) * grad_hidden, axis=1)
    grad_gate = grad_hidden * up_pre * sigmoid_gate * (1.0 + gate_pre * (1.0 - sigmoid_gate))
    grad_up = grad_hidden * silu_gate
    grad_cache = jnp.stack([grad_gate, grad_up]).astype(jnp.bfloat16)
    return (grad_cache, scores)


def placement(flat_ids, slots, places):
    count_all = flat_ids.shape[0]
    row_index = lax.broadcasted_iota(jnp.int32, (count_all, count_all), 0)
    col_index = lax.broadcasted_iota(jnp.int32, (count_all, count_all), 1)
    before = jnp.logical_and(flat_ids[:, None] == flat_ids[None, :], col_index < row_index)
    slot_rank = jnp.sum(before.astype(jnp.int32), axis=1)
    target = flat_ids * slots + slot_rank
    return lax.broadcasted_iota(jnp.int32, (places, count_all), 0) == target[None, :]


def on_device(out_grad, gate_probs, copy_ids, copy_expert, w_down, swiglu_in):
    n_data = lax.axis_size("dp")
    n_expert = lax.axis_size("expert")
    cache = swiglu_in[0]
    weight = w_down[0]
    rows_all = cache.shape[1]
    hidden_dev = cache.shape[2]
    slots = rows_all // (n_data * n_expert)
    places = n_expert * slots
    width = out_grad.shape[1]
    tok_dev = out_grad.shape[0]
    top_count = copy_ids.shape[1]
    pair_count = tok_dev * top_count
    weighted = gate_probs.astype(jnp.float32)[:, :, None] * out_grad.astype(jnp.float32)[:, None, :]
    weighted = weighted.reshape(pair_count, width).astype(jnp.bfloat16)
    placing = placement(copy_ids.reshape(pair_count), slots, places)
    outgoing = jnp.dot(
        placing.astype(jnp.bfloat16), weighted, preferred_element_type=jnp.float32
    ).astype(jnp.bfloat16)
    outgoing = outgoing.reshape(n_expert, slots, width)
    parts = activations(cache)
    hidden = parts[0]
    chunk = width // CHUNKS
    grad_hidden = None
    col_parts = []
    for k in range(CHUNKS):
        send = outgoing[:, :, k * chunk:(k + 1) * chunk]
        arrived = lax.all_to_all(send, "expert", split_axis=0, concat_axis=0, tiled=True)
        rows_part = arrived.reshape(places, chunk)
        piece = lax.all_gather(rows_part, "dp", axis=0, tiled=True)
        part = lax.dot_general(
            piece, weight[:, k * chunk:(k + 1) * chunk], (((1,), (1,)), ((), ())),
            preferred_element_type=jnp.float32,
        )
        grad_hidden = part if grad_hidden is None else grad_hidden + part
        columns = lax.dot_general(
            hidden, piece, (((0,), (0,)), ((), ())), preferred_element_type=jnp.float32
        )
        col_parts.append(columns.astype(jnp.bfloat16))
    grad_cache, scores = finish(grad_hidden, parts)
    copy_grad = jnp.concatenate(col_parts, axis=1)
    same_expert = (copy_expert[:, None] == copy_expert[None, :]).astype(jnp.float32)
    block = width // n_expert
    feature_blocks = copy_grad.reshape(hidden_dev, n_expert, block)
    summed = jnp.einsum(
        "ab,nbd->and",
        same_expert,
        lax.all_to_all(feature_blocks, "expert", split_axis=1, concat_axis=1, tiled=True).astype(
            jnp.float32
        ),
        precision=lax.Precision.HIGHEST,
    ).astype(jnp.bfloat16)
    partial_scores = scores.reshape(n_data, places)
    row_scores = jnp.sum(
        lax.all_to_all(partial_scores, "dp", split_axis=0, concat_axis=0, tiled=True), axis=0
    ).reshape(n_expert, slots)
    high = row_scores.astype(jnp.bfloat16)
    rest = row_scores - high.astype(jnp.float32)
    mid = rest.astype(jnp.bfloat16)
    low = (rest - mid.astype(jnp.float32)).astype(jnp.bfloat16)
    score_terms = jnp.concatenate([high, mid, low], axis=1)
    pad = jnp.zeros((n_expert, 128 - 3 * slots), jnp.bfloat16)
    outbound = jnp.concatenate(
        [summed.reshape(n_expert, hidden_dev * block), score_terms, pad], axis=1
    )
    inbound = lax.all_to_all(outbound, "expert", split_axis=0, concat_axis=0, tiled=True)
    joined = inbound[:, : hidden_dev * block].reshape(n_expert, hidden_dev, block)
    joined = joined.transpose(1, 0, 2)
    terms = inbound[:, hidden_dev * block : hidden_dev * block + 3 * slots].astype(jnp.float32)
    score_back = (
        terms[:, :slots] + terms[:, slots : 2 * slots] + terms[:, 2 * slots :]
    ).reshape(places)
    assigned_score = jnp.dot(
        placing.astype(jnp.float32).T, score_back, precision=lax.Precision.HIGHEST
    )
    grad_probs = (assigned_score / gate_probs.reshape(-1).astype(jnp.float32)).reshape(
        gate_probs.shape
    )
    grad_weight = joined.reshape(1, hidden_dev, width)
    return (grad_cache[None], grad_weight, grad_probs)


def solution(mesh):
    placed = (
        P(("dp", "expert"), None),
        P(("dp", "expert"), None),
        P(("dp", "expert"), None),
        P(),
        P("expert", "dp", None),
        P("expert", None, None, "dp"),
    )
    return jax.shard_map(
        on_device,
        mesh=mesh,
        in_specs=placed,
        out_specs=(
            P("expert", None, None, "dp"),
            P("expert", "dp", None),
            P(("dp", "expert"), None),
        ),
        check_vma=False,
    )
```

```python
import jax
import jax.numpy as jnp
from jax import lax
from jax.sharding import PartitionSpec as P

CHUNKS = 1


def activations(cache):
    gate_pre = cache[0].astype(jnp.float32)
    up_pre = cache[1].astype(jnp.float32)
    sigmoid_gate = jax.nn.sigmoid(gate_pre)
    silu_gate = gate_pre * sigmoid_gate
    hidden = (silu_gate * up_pre).astype(jnp.bfloat16)
    return (hidden, gate_pre, up_pre, sigmoid_gate, silu_gate)


def finish(grad_hidden, parts):
    hidden, gate_pre, up_pre, sigmoid_gate, silu_gate = parts
    scores = jnp.sum(hidden.astype(jnp.float32) * grad_hidden, axis=1)
    grad_gate = grad_hidden * up_pre * sigmoid_gate * (1.0 + gate_pre * (1.0 - sigmoid_gate))
    grad_up = grad_hidden * silu_gate
    grad_cache = jnp.stack([grad_gate, grad_up]).astype(jnp.bfloat16)
    return (grad_cache, scores)


def placement(flat_ids, slots, places):
    count_all = flat_ids.shape[0]
    row_index = lax.broadcasted_iota(jnp.int32, (count_all, count_all), 0)
    col_index = lax.broadcasted_iota(jnp.int32, (count_all, count_all), 1)
    before = jnp.logical_and(flat_ids[:, None] == flat_ids[None, :], col_index < row_index)
    slot_rank = jnp.sum(before.astype(jnp.int32), axis=1)
    target = flat_ids * slots + slot_rank
    return lax.broadcasted_iota(jnp.int32, (places, count_all), 0) == target[None, :]


def on_device(out_grad, gate_probs, copy_ids, copy_expert, w_down, swiglu_in):
    n_data = lax.axis_size("dp")
    n_expert = lax.axis_size("expert")
    cache = swiglu_in[0]
    weight = w_down[0]
    rows_all = cache.shape[1]
    hidden_dev = cache.shape[2]
    slots = rows_all // (n_data * n_expert)
    places = n_expert * slots
    width = out_grad.shape[1]
    tok_dev = out_grad.shape[0]
    top_count = copy_ids.shape[1]
    pair_count = tok_dev * top_count
    weighted = gate_probs.astype(jnp.float32)[:, :, None] * out_grad.astype(jnp.float32)[:, None, :]
    weighted = weighted.reshape(pair_count, width).astype(jnp.bfloat16)
    placing = placement(copy_ids.reshape(pair_count), slots, places)
    outgoing = jnp.dot(
        placing.astype(jnp.bfloat16), weighted, preferred_element_type=jnp.float32
    ).astype(jnp.bfloat16)
    outgoing = outgoing.reshape(n_expert, slots, width)
    parts = activations(cache)
    hidden = parts[0]
    chunk = width // CHUNKS
    grad_hidden = None
    col_parts = []
    for k in range(CHUNKS):
        send = outgoing[:, :, k * chunk:(k + 1) * chunk]
        lanes = 128 if (slots * chunk) % 128 == 0 else chunk
        send = send.reshape(n_expert, slots * chunk // lanes, lanes)
        arrived = lax.all_to_all(send, "expert", split_axis=0, concat_axis=0, tiled=True)
        rows_part = arrived.reshape(places, chunk)
        piece = lax.all_gather(rows_part, "dp", axis=0, tiled=True)
        part = lax.dot_general(
            piece, weight[:, k * chunk:(k + 1) * chunk], (((1,), (1,)), ((), ())),
            preferred_element_type=jnp.float32,
        )
        grad_hidden = part if grad_hidden is None else grad_hidden + part
        columns = lax.dot_general(
            hidden, piece, (((0,), (0,)), ((), ())), preferred_element_type=jnp.float32
        )
        col_parts.append(columns.astype(jnp.bfloat16))
    grad_cache, scores = finish(grad_hidden, parts)
    copy_grad = jnp.concatenate(col_parts, axis=1)
    same_expert = (copy_expert[:, None] == copy_expert[None, :]).astype(jnp.float32)
    block = width // n_expert
    feature_blocks = copy_grad.reshape(hidden_dev, n_expert, block)
    summed = jnp.einsum(
        "ab,nbd->and",
        same_expert,
        lax.all_to_all(feature_blocks, "expert", split_axis=1, concat_axis=1, tiled=True).astype(
            jnp.float32
        ),
        precision=lax.Precision.HIGHEST,
    ).astype(jnp.bfloat16)
    partial_scores = scores.reshape(n_data, places)
    row_scores = jnp.sum(
        lax.all_to_all(partial_scores, "dp", split_axis=0, concat_axis=0, tiled=True), axis=0
    ).reshape(n_expert, slots)
    high = row_scores.astype(jnp.bfloat16)
    rest = row_scores - high.astype(jnp.float32)
    mid = rest.astype(jnp.bfloat16)
    low = (rest - mid.astype(jnp.float32)).astype(jnp.bfloat16)
    score_terms = jnp.concatenate([high, mid, low], axis=1)
    pad = jnp.zeros((n_expert, 128 - 3 * slots), jnp.bfloat16)
    outbound = jnp.concatenate(
        [summed.reshape(n_expert, hidden_dev * block), score_terms, pad], axis=1
    )
    inbound = lax.all_to_all(outbound, "expert", split_axis=0, concat_axis=0, tiled=True)
    joined = inbound[:, : hidden_dev * block].reshape(n_expert, hidden_dev, block)
    joined = joined.transpose(1, 0, 2)
    terms = inbound[:, hidden_dev * block : hidden_dev * block + 3 * slots].astype(jnp.float32)
    score_back = (
        terms[:, :slots] + terms[:, slots : 2 * slots] + terms[:, 2 * slots :]
    ).reshape(places)
    assigned_score = jnp.dot(
        placing.astype(jnp.float32).T, score_back, precision=lax.Precision.HIGHEST
    )
    grad_probs = (assigned_score / gate_probs.reshape(-1).astype(jnp.float32)).reshape(
        gate_probs.shape
    )
    grad_weight = joined.reshape(1, hidden_dev, width)
    return (grad_cache[None], grad_weight, grad_probs)


def solution(mesh):
    placed = (
        P(("dp", "expert"), None),
        P(("dp", "expert"), None),
        P(("dp", "expert"), None),
        P(),
        P("expert", "dp", None),
        P("expert", None, None, "dp"),
    )
    return jax.shard_map(
        on_device,
        mesh=mesh,
        in_specs=placed,
        out_specs=(
            P("expert", None, None, "dp"),
            P("expert", "dp", None),
            P(("dp", "expert"), None),
        ),
        check_vma=False,
    )
```

```python
import jax
import jax.numpy as jnp
from jax import lax
from jax.sharding import PartitionSpec as P

CHUNKS = 1


def activations(cache):
    gate_pre = cache[0].astype(jnp.float32)
    up_pre = cache[1].astype(jnp.float32)
    sigmoid_gate = jax.nn.sigmoid(gate_pre)
    silu_gate = gate_pre * sigmoid_gate
    hidden = (silu_gate * up_pre).astype(jnp.bfloat16)
    return (hidden, gate_pre, up_pre, sigmoid_gate, silu_gate)


def finish(grad_hidden, parts):
    hidden, gate_pre, up_pre, sigmoid_gate, silu_gate = parts
    scores = jnp.sum(hidden.astype(jnp.float32) * grad_hidden, axis=1)
    grad_gate = grad_hidden * up_pre * sigmoid_gate * (1.0 + gate_pre * (1.0 - sigmoid_gate))
    grad_up = grad_hidden * silu_gate
    grad_cache = jnp.stack([grad_gate, grad_up]).astype(jnp.bfloat16)
    return (grad_cache, scores)


def placement(flat_ids, slots, places):
    count_all = flat_ids.shape[0]
    row_index = lax.broadcasted_iota(jnp.int32, (count_all, count_all), 0)
    col_index = lax.broadcasted_iota(jnp.int32, (count_all, count_all), 1)
    before = jnp.logical_and(flat_ids[:, None] == flat_ids[None, :], col_index < row_index)
    slot_rank = jnp.sum(before.astype(jnp.int32), axis=1)
    target = flat_ids * slots + slot_rank
    return lax.broadcasted_iota(jnp.int32, (places, count_all), 0) == target[None, :]


def on_device(out_grad, gate_probs, copy_ids, copy_expert, w_down, swiglu_in):
    n_data = lax.axis_size("dp")
    n_expert = lax.axis_size("expert")
    cache = swiglu_in[0]
    weight = w_down[0]
    rows_all = cache.shape[1]
    hidden_dev = cache.shape[2]
    slots = rows_all // (n_data * n_expert)
    places = n_expert * slots
    width = out_grad.shape[1]
    tok_dev = out_grad.shape[0]
    top_count = copy_ids.shape[1]
    pair_count = tok_dev * top_count
    weighted = gate_probs.astype(jnp.float32)[:, :, None] * out_grad.astype(jnp.float32)[:, None, :]
    weighted = weighted.reshape(pair_count, width).astype(jnp.bfloat16)
    placing = placement(copy_ids.reshape(pair_count), slots, places)
    outgoing = jnp.dot(
        placing.astype(jnp.bfloat16), weighted, preferred_element_type=jnp.float32
    ).astype(jnp.bfloat16)
    outgoing = outgoing.reshape(n_expert, slots, width)
    parts = activations(cache)
    hidden = parts[0]
    chunk = width // CHUNKS
    grad_hidden = None
    col_parts = []
    for k in range(CHUNKS):
        send = outgoing[:, :, k * chunk:(k + 1) * chunk]
        lanes = 128 if (slots * chunk) % 128 == 0 else chunk
        send = send.reshape(n_expert, slots * chunk // lanes, lanes)
        arrived = lax.all_to_all(send, "expert", split_axis=0, concat_axis=0, tiled=True)
        rows_part = arrived.reshape(places, chunk)
        piece = lax.all_gather(rows_part, "dp", axis=0, tiled=True)
        part = lax.dot_general(
            piece, weight[:, k * chunk:(k + 1) * chunk], (((1,), (1,)), ((), ())),
            preferred_element_type=jnp.float32,
        )
        grad_hidden = part if grad_hidden is None else grad_hidden + part
        columns = lax.dot_general(
            hidden, piece, (((0,), (0,)), ((), ())), preferred_element_type=jnp.float32
        )
        col_parts.append(columns.astype(jnp.bfloat16))
    grad_cache, scores = finish(grad_hidden, parts)
    copy_grad = jnp.concatenate(col_parts, axis=1)
    share = hidden_dev // n_expert
    blocks = copy_grad.reshape(n_expert, share, width)
    gathered = lax.all_to_all(blocks, "expert", split_axis=0, concat_axis=0, tiled=True)
    same_expert = (copy_expert[:, None] == copy_expert[None, :]).astype(jnp.bfloat16)
    summed = jnp.dot(
        same_expert, gathered.reshape(n_expert, share * width), preferred_element_type=jnp.float32
    ).astype(jnp.bfloat16).reshape(n_expert, share, width)
    partial_scores = scores.reshape(n_data, places)
    row_scores = jnp.sum(
        lax.all_to_all(partial_scores, "dp", split_axis=0, concat_axis=0, tiled=True), axis=0
    ).reshape(n_expert, slots)
    high = row_scores.astype(jnp.bfloat16)
    rest = row_scores - high.astype(jnp.float32)
    mid = rest.astype(jnp.bfloat16)
    low = (rest - mid.astype(jnp.float32)).astype(jnp.bfloat16)
    extra = 128
    first = jnp.concatenate(
        [high, mid, low, jnp.zeros((n_expert, extra - 3 * slots), jnp.bfloat16)], axis=1
    )
    tail = jnp.concatenate(
        [first[:, None, :], jnp.zeros((n_expert, share - 1, extra), jnp.bfloat16)], axis=1
    )
    outbound = jnp.concatenate([summed, tail], axis=2)
    inbound = lax.all_to_all(outbound, "expert", split_axis=0, concat_axis=0, tiled=True)
    grad_weight = inbound[:, :, :width].reshape(1, hidden_dev, width)
    terms = inbound[:, 0, width : width + 3 * slots].astype(jnp.float32)
    score_back = (
        terms[:, :slots] + terms[:, slots : 2 * slots] + terms[:, 2 * slots :]
    ).reshape(places)
    assigned_score = jnp.dot(
        placing.astype(jnp.float32).T, score_back, precision=lax.Precision.HIGHEST
    )
    grad_probs = (assigned_score / gate_probs.reshape(-1).astype(jnp.float32)).reshape(
        gate_probs.shape
    )
    return (grad_cache[None], grad_weight, grad_probs)


def solution(mesh):
    placed = (
        P(("dp", "expert"), None),
        P(("dp", "expert"), None),
        P(("dp", "expert"), None),
        P(),
        P("expert", "dp", None),
        P("expert", None, None, "dp"),
    )
    return jax.shard_map(
        on_device,
        mesh=mesh,
        in_specs=placed,
        out_specs=(
            P("expert", None, None, "dp"),
            P("expert", "dp", None),
            P(("dp", "expert"), None),
        ),
        check_vma=False,
    )
```

```python
import jax
import jax.numpy as jnp
from jax import lax
from jax.sharding import PartitionSpec as P

def activations(cache):
    gate_pre = cache[0].astype(jnp.float32)
    up_pre = cache[1].astype(jnp.float32)
    sigmoid_gate = jax.nn.sigmoid(gate_pre)
    silu_gate = gate_pre * sigmoid_gate
    hidden = (silu_gate * up_pre).astype(jnp.bfloat16)
    return (hidden, gate_pre, up_pre, sigmoid_gate, silu_gate)


def finish(grad_hidden, parts):
    hidden, gate_pre, up_pre, sigmoid_gate, silu_gate = parts
    scores = jnp.sum(hidden.astype(jnp.float32) * grad_hidden, axis=1)
    grad_gate = grad_hidden * up_pre * sigmoid_gate * (1.0 + gate_pre * (1.0 - sigmoid_gate))
    grad_up = grad_hidden * silu_gate
    grad_cache = jnp.stack([grad_gate, grad_up]).astype(jnp.bfloat16)
    return (grad_cache, scores)


def placement(flat_ids, slots, places):
    count_all = flat_ids.shape[0]
    row_index = lax.broadcasted_iota(jnp.int32, (count_all, count_all), 0)
    col_index = lax.broadcasted_iota(jnp.int32, (count_all, count_all), 1)
    before = jnp.logical_and(flat_ids[:, None] == flat_ids[None, :], col_index < row_index)
    slot_rank = jnp.sum(before.astype(jnp.int32), axis=1)
    target = flat_ids * slots + slot_rank
    return lax.broadcasted_iota(jnp.int32, (places, count_all), 0) == target[None, :]


def on_device(out_grad, gate_probs, copy_ids, copy_expert, w_down, swiglu_in):
    n_data = lax.axis_size("dp")
    n_expert = lax.axis_size("expert")
    cache = swiglu_in[0]
    weight = w_down[0]
    rows_all = cache.shape[1]
    hidden_dev = cache.shape[2]
    slots = rows_all // (n_data * n_expert)
    places = n_expert * slots
    width = out_grad.shape[1]
    tok_dev = out_grad.shape[0]
    top_count = copy_ids.shape[1]
    pair_count = tok_dev * top_count
    weighted = gate_probs.astype(jnp.float32)[:, :, None] * out_grad.astype(jnp.float32)[:, None, :]
    weighted = weighted.reshape(pair_count, width).astype(jnp.bfloat16)
    placing = placement(copy_ids.reshape(pair_count), slots, places)
    outgoing = jnp.dot(
        placing.astype(jnp.bfloat16), weighted, preferred_element_type=jnp.float32
    ).astype(jnp.bfloat16)
    outgoing = outgoing.reshape(n_expert, slots, width)
    parts = activations(cache)
    hidden = parts[0]
    lanes = 128 if (slots * width) % 128 == 0 else width
    send = outgoing.reshape(n_expert, slots * width // lanes, lanes)
    arrived = lax.all_to_all(send, "expert", split_axis=0, concat_axis=0, tiled=True)
    rows_part = arrived.reshape(places, width)
    me = lax.axis_index("dp")
    hidden_rel = jnp.roll(hidden.reshape(n_data, places, hidden_dev), -me, axis=0)
    forward = [(j, (j + 1) % n_data) for j in range(n_data)]
    backward = [(j, (j - 1) % n_data) for j in range(n_data)]
    grad_rel = [None] * n_data
    copy_acc = None

    def take(r, rows):
        nonlocal copy_acc
        grad_rel[r] = lax.dot_general(
            rows, weight, (((1,), (1,)), ((), ())), preferred_element_type=jnp.float32
        )
        term = lax.dot_general(
            hidden_rel[r], rows, (((0,), (0,)), ((), ())), preferred_element_type=jnp.float32
        )
        copy_acc = term if copy_acc is None else copy_acc + term

    take(0, rows_part)
    ahead = rows_part
    behind = rows_part
    for step in range(1, n_data // 2 + 1):
        ahead = lax.ppermute(ahead, "dp", forward)
        if step < n_data - step:
            behind = lax.ppermute(behind, "dp", backward)
        take((-step) % n_data, ahead)
        if step < n_data - step:
            take(step, behind)
    grad_hidden = jnp.roll(jnp.stack(grad_rel), me, axis=0).reshape(rows_all, hidden_dev)
    col_parts = [copy_acc.astype(jnp.bfloat16)]
    grad_cache, scores = finish(grad_hidden, parts)
    copy_grad = jnp.concatenate(col_parts, axis=1)
    share = hidden_dev // n_expert
    blocks = copy_grad.reshape(n_expert, share, width)
    gathered = lax.all_to_all(blocks, "expert", split_axis=0, concat_axis=0, tiled=True)
    same_expert = (copy_expert[:, None] == copy_expert[None, :]).astype(jnp.bfloat16)
    summed = jnp.dot(
        same_expert, gathered.reshape(n_expert, share * width), preferred_element_type=jnp.float32
    ).astype(jnp.bfloat16).reshape(n_expert, share, width)
    partial_scores = scores.reshape(n_data, places)
    row_scores = jnp.sum(
        lax.all_to_all(partial_scores, "dp", split_axis=0, concat_axis=0, tiled=True), axis=0
    ).reshape(n_expert, slots)
    high = row_scores.astype(jnp.bfloat16)
    rest = row_scores - high.astype(jnp.float32)
    mid = rest.astype(jnp.bfloat16)
    low = (rest - mid.astype(jnp.float32)).astype(jnp.bfloat16)
    extra = 128
    first = jnp.concatenate(
        [high, mid, low, jnp.zeros((n_expert, extra - 3 * slots), jnp.bfloat16)], axis=1
    )
    tail = jnp.concatenate(
        [first[:, None, :], jnp.zeros((n_expert, share - 1, extra), jnp.bfloat16)], axis=1
    )
    outbound = jnp.concatenate([summed, tail], axis=2)
    inbound = lax.all_to_all(outbound, "expert", split_axis=0, concat_axis=0, tiled=True)
    grad_weight = inbound[:, :, :width].reshape(1, hidden_dev, width)
    terms = inbound[:, 0, width : width + 3 * slots].astype(jnp.float32)
    score_back = (
        terms[:, :slots] + terms[:, slots : 2 * slots] + terms[:, 2 * slots :]
    ).reshape(places)
    assigned_score = jnp.dot(
        placing.astype(jnp.float32).T, score_back, precision=lax.Precision.HIGHEST
    )
    grad_probs = (assigned_score / gate_probs.reshape(-1).astype(jnp.float32)).reshape(
        gate_probs.shape
    )
    return (grad_cache[None], grad_weight, grad_probs)


def solution(mesh):
    placed = (
        P(("dp", "expert"), None),
        P(("dp", "expert"), None),
        P(("dp", "expert"), None),
        P(),
        P("expert", "dp", None),
        P("expert", None, None, "dp"),
    )
    return jax.shard_map(
        on_device,
        mesh=mesh,
        in_specs=placed,
        out_specs=(
            P("expert", None, None, "dp"),
            P("expert", "dp", None),
            P(("dp", "expert"), None),
        ),
        check_vma=False,
    )
```

```python
import jax
import jax.numpy as jnp
from jax import lax
from jax.sharding import PartitionSpec as P

def activations(cache):
    gate_pre = cache[0].astype(jnp.float32)
    up_pre = cache[1].astype(jnp.float32)
    sigmoid_gate = jax.nn.sigmoid(gate_pre)
    silu_gate = gate_pre * sigmoid_gate
    hidden = (silu_gate * up_pre).astype(jnp.bfloat16)
    return (hidden, gate_pre, up_pre, sigmoid_gate, silu_gate)


def finish(grad_hidden, parts):
    hidden, gate_pre, up_pre, sigmoid_gate, silu_gate = parts
    scores = jnp.sum(hidden.astype(jnp.float32) * grad_hidden, axis=1)
    grad_gate = grad_hidden * up_pre * sigmoid_gate * (1.0 + gate_pre * (1.0 - sigmoid_gate))
    grad_up = grad_hidden * silu_gate
    grad_cache = jnp.stack([grad_gate, grad_up]).astype(jnp.bfloat16)
    return (grad_cache, scores)


def placement(flat_ids, slots, places):
    count_all = flat_ids.shape[0]
    row_index = lax.broadcasted_iota(jnp.int32, (count_all, count_all), 0)
    col_index = lax.broadcasted_iota(jnp.int32, (count_all, count_all), 1)
    before = jnp.logical_and(flat_ids[:, None] == flat_ids[None, :], col_index < row_index)
    slot_rank = jnp.sum(before.astype(jnp.int32), axis=1)
    target = flat_ids * slots + slot_rank
    return lax.broadcasted_iota(jnp.int32, (places, count_all), 0) == target[None, :]


def on_device(out_grad, gate_probs, copy_ids, copy_expert, w_down, swiglu_in):
    n_data = lax.axis_size("dp")
    n_expert = lax.axis_size("expert")
    cache = swiglu_in[0]
    weight = w_down[0]
    rows_all = cache.shape[1]
    hidden_dev = cache.shape[2]
    slots = rows_all // (n_data * n_expert)
    places = n_expert * slots
    width = out_grad.shape[1]
    tok_dev = out_grad.shape[0]
    top_count = copy_ids.shape[1]
    pair_count = tok_dev * top_count
    weighted = gate_probs.astype(jnp.float32)[:, :, None] * out_grad.astype(jnp.float32)[:, None, :]
    weighted = weighted.reshape(pair_count, width).astype(jnp.bfloat16)
    placing = placement(copy_ids.reshape(pair_count), slots, places)
    outgoing = jnp.dot(
        placing.astype(jnp.bfloat16), weighted, preferred_element_type=jnp.float32
    ).astype(jnp.bfloat16)
    outgoing = outgoing.reshape(n_expert, slots, width)
    parts = activations(cache)
    hidden = parts[0]
    lanes = 128 if (slots * width) % 128 == 0 else width
    send = outgoing.reshape(n_expert, slots * width // lanes, lanes)
    arrived = lax.all_to_all(send, "expert", split_axis=0, concat_axis=0, tiled=True)
    rows_part = arrived.reshape(places, width)
    me = lax.axis_index("dp")
    hidden_blocks = hidden.reshape(n_data, places, hidden_dev)
    grad_blocks = jnp.zeros((n_data, places, hidden_dev), jnp.float32)
    copy_acc = None

    def take(k, rows):
        nonlocal copy_acc, grad_blocks
        part = lax.dot_general(
            rows, weight, (((1,), (1,)), ((), ())), preferred_element_type=jnp.float32
        )
        grad_blocks = lax.dynamic_update_index_in_dim(grad_blocks, part, k, 0)
        own_hidden = lax.dynamic_index_in_dim(hidden_blocks, k, 0, keepdims=False)
        term = lax.dot_general(
            own_hidden, rows, (((0,), (0,)), ((), ())), preferred_element_type=jnp.float32
        )
        copy_acc = term if copy_acc is None else copy_acc + term

    take(me, rows_part)
    if n_data == 8:
        chips = n_data // 2
        y = me // 2
        core = me % 2
        swap = [(j, j ^ 1) for j in range(n_data)]
        shift = [(2 * t, 2 * ((t + 1) % chips)) for t in range(chips)] + [
            (2 * t + 1, 2 * ((t - 1) % chips) + 1) for t in range(chips)
        ]
        partner = lax.ppermute(rows_part, "dp", swap)
        take(me ^ 1, partner)
        near_own = lax.ppermute(rows_part, "dp", shift)
        near_partner = lax.ppermute(partner, "dp", shift)
        src_near = jnp.where(core == 0, 2 * ((y - 1) % chips), 2 * ((y + 1) % chips) + 1)
        take(src_near, near_own)
        take(src_near ^ 1, near_partner)
        side_own = lax.ppermute(near_own, "dp", swap)
        side_partner = lax.ppermute(near_partner, "dp", swap)
        src_side = jnp.where(core == 0, 2 * ((y + 1) % chips) + 1, 2 * ((y - 1) % chips))
        take(src_side, side_own)
        take(src_side ^ 1, side_partner)
        far = lax.ppermute(near_own, "dp", shift)
        src_far = jnp.where(core == 0, 2 * ((y - 2) % chips), 2 * ((y + 2) % chips) + 1)
        take(src_far, far)
        far_side = lax.ppermute(far, "dp", swap)
        take(src_far ^ 1, far_side)
    else:
        forward = [(j, (j + 1) % n_data) for j in range(n_data)]
        ahead = rows_part
        for step in range(1, n_data):
            ahead = lax.ppermute(ahead, "dp", forward)
            take((me - step) % n_data, ahead)
    grad_hidden = grad_blocks.reshape(rows_all, hidden_dev)
    col_parts = [copy_acc.astype(jnp.bfloat16)]
    grad_cache, scores = finish(grad_hidden, parts)
    copy_grad = jnp.concatenate(col_parts, axis=1)
    share = hidden_dev // n_expert
    blocks = copy_grad.reshape(n_expert, share, width)
    gathered = lax.all_to_all(blocks, "expert", split_axis=0, concat_axis=0, tiled=True)
    same_expert = (copy_expert[:, None] == copy_expert[None, :]).astype(jnp.bfloat16)
    summed = jnp.dot(
        same_expert, gathered.reshape(n_expert, share * width), preferred_element_type=jnp.float32
    ).astype(jnp.bfloat16).reshape(n_expert, share, width)
    partial_scores = scores.reshape(n_data, places)
    row_scores = jnp.sum(
        lax.all_to_all(partial_scores, "dp", split_axis=0, concat_axis=0, tiled=True), axis=0
    ).reshape(n_expert, slots)
    high = row_scores.astype(jnp.bfloat16)
    rest = row_scores - high.astype(jnp.float32)
    mid = rest.astype(jnp.bfloat16)
    low = (rest - mid.astype(jnp.float32)).astype(jnp.bfloat16)
    extra = 128
    first = jnp.concatenate(
        [high, mid, low, jnp.zeros((n_expert, extra - 3 * slots), jnp.bfloat16)], axis=1
    )
    tail = jnp.concatenate(
        [first[:, None, :], jnp.zeros((n_expert, share - 1, extra), jnp.bfloat16)], axis=1
    )
    outbound = jnp.concatenate([summed, tail], axis=2)
    inbound = lax.all_to_all(outbound, "expert", split_axis=0, concat_axis=0, tiled=True)
    grad_weight = inbound[:, :, :width].reshape(1, hidden_dev, width)
    terms = inbound[:, 0, width : width + 3 * slots].astype(jnp.float32)
    score_back = (
        terms[:, :slots] + terms[:, slots : 2 * slots] + terms[:, 2 * slots :]
    ).reshape(places)
    assigned_score = jnp.dot(
        placing.astype(jnp.float32).T, score_back, precision=lax.Precision.HIGHEST
    )
    grad_probs = (assigned_score / gate_probs.reshape(-1).astype(jnp.float32)).reshape(
        gate_probs.shape
    )
    return (grad_cache[None], grad_weight, grad_probs)


def solution(mesh):
    placed = (
        P(("dp", "expert"), None),
        P(("dp", "expert"), None),
        P(("dp", "expert"), None),
        P(),
        P("expert", "dp", None),
        P("expert", None, None, "dp"),
    )
    return jax.shard_map(
        on_device,
        mesh=mesh,
        in_specs=placed,
        out_specs=(
            P("expert", None, None, "dp"),
            P("expert", "dp", None),
            P(("dp", "expert"), None),
        ),
        check_vma=False,
    )
```

```python
import jax
import jax.numpy as jnp
from jax import lax
from jax.sharding import PartitionSpec as P

def activations(cache):
    gate_pre = cache[0].astype(jnp.float32)
    up_pre = cache[1].astype(jnp.float32)
    sigmoid_gate = jax.nn.sigmoid(gate_pre)
    silu_gate = gate_pre * sigmoid_gate
    hidden = (silu_gate * up_pre).astype(jnp.bfloat16)
    return (hidden, gate_pre, up_pre, sigmoid_gate, silu_gate)


def finish(grad_hidden, parts):
    hidden, gate_pre, up_pre, sigmoid_gate, silu_gate = parts
    scores = jnp.sum(hidden.astype(jnp.float32) * grad_hidden, axis=1)
    grad_gate = grad_hidden * up_pre * sigmoid_gate * (1.0 + gate_pre * (1.0 - sigmoid_gate))
    grad_up = grad_hidden * silu_gate
    grad_cache = jnp.stack([grad_gate, grad_up]).astype(jnp.bfloat16)
    return (grad_cache, scores)


def placement(flat_ids, slots, places):
    count_all = flat_ids.shape[0]
    row_index = lax.broadcasted_iota(jnp.int32, (count_all, count_all), 0)
    col_index = lax.broadcasted_iota(jnp.int32, (count_all, count_all), 1)
    before = jnp.logical_and(flat_ids[:, None] == flat_ids[None, :], col_index < row_index)
    slot_rank = jnp.sum(before.astype(jnp.int32), axis=1)
    target = flat_ids * slots + slot_rank
    return lax.broadcasted_iota(jnp.int32, (places, count_all), 0) == target[None, :]


def gather_rows(rows_part, take, me, n_data):
    take(me, rows_part)
    if n_data == 8:
        chips = n_data // 2
        y = me // 2
        core = me % 2
        swap = [(j, j ^ 1) for j in range(n_data)]
        shift = [(2 * t, 2 * ((t + 1) % chips)) for t in range(chips)] + [
            (2 * t + 1, 2 * ((t - 1) % chips) + 1) for t in range(chips)
        ]
        partner = lax.ppermute(rows_part, "dp", swap)
        take(me ^ 1, partner)
        near_own = lax.ppermute(rows_part, "dp", shift)
        near_partner = lax.ppermute(partner, "dp", shift)
        src_near = jnp.where(core == 0, 2 * ((y - 1) % chips), 2 * ((y + 1) % chips) + 1)
        take(src_near, near_own)
        take(src_near ^ 1, near_partner)
        side_own = lax.ppermute(near_own, "dp", swap)
        side_partner = lax.ppermute(near_partner, "dp", swap)
        src_side = jnp.where(core == 0, 2 * ((y + 1) % chips) + 1, 2 * ((y - 1) % chips))
        take(src_side, side_own)
        take(src_side ^ 1, side_partner)
        far = lax.ppermute(near_own, "dp", shift)
        src_far = jnp.where(core == 0, 2 * ((y - 2) % chips), 2 * ((y + 2) % chips) + 1)
        take(src_far, far)
        far_side = lax.ppermute(far, "dp", swap)
        take(src_far ^ 1, far_side)
    else:
        forward = [(j, (j + 1) % n_data) for j in range(n_data)]
        ahead = rows_part
        for step in range(1, n_data):
            ahead = lax.ppermute(ahead, "dp", forward)
            take((me - step) % n_data, ahead)


def on_device(out_grad, gate_probs, copy_ids, copy_expert, w_down, swiglu_in):
    n_data = lax.axis_size("dp")
    n_expert = lax.axis_size("expert")
    cache = swiglu_in[0]
    weight = w_down[0]
    rows_all = cache.shape[1]
    hidden_dev = cache.shape[2]
    slots = rows_all // (n_data * n_expert)
    places = n_expert * slots
    width = out_grad.shape[1]
    tok_dev = out_grad.shape[0]
    top_count = copy_ids.shape[1]
    pair_count = tok_dev * top_count
    weighted = gate_probs.astype(jnp.float32)[:, :, None] * out_grad.astype(jnp.float32)[:, None, :]
    weighted = weighted.reshape(pair_count, width).astype(jnp.bfloat16)
    placing = placement(copy_ids.reshape(pair_count), slots, places)
    outgoing = jnp.dot(
        placing.astype(jnp.bfloat16), weighted, preferred_element_type=jnp.float32
    ).astype(jnp.bfloat16)
    outgoing = outgoing.reshape(n_expert, slots, width)
    parts = activations(cache)
    hidden = parts[0]
    me = lax.axis_index("dp")
    hidden_blocks = hidden.reshape(n_data, n_expert, slots, hidden_dev)
    grad_blocks = jnp.zeros((n_data, n_expert, slots, hidden_dev), jnp.float32)
    copy_acc = None
    bounds = [(0, slots - 1), (slots - 1, slots)] if slots > 1 else [(0, slots)]
    for lo, hi in bounds:
        count = hi - lo
        lanes = 128 if (count * width) % 128 == 0 else width
        send = outgoing[:, lo:hi, :].reshape(n_expert, count * width // lanes, lanes)
        arrived = lax.all_to_all(send, "expert", split_axis=0, concat_axis=0, tiled=True)
        rows_part = arrived.reshape(n_expert * count, width)

        def take(k, rows, lo=lo, hi=hi, count=count):
            nonlocal copy_acc, grad_blocks
            part = lax.dot_general(
                rows, weight, (((1,), (1,)), ((), ())), preferred_element_type=jnp.float32
            )
            grad_blocks = lax.dynamic_update_slice(
                grad_blocks, part.reshape(1, n_expert, count, hidden_dev), (k, 0, lo, 0)
            )
            own_hidden = lax.dynamic_index_in_dim(hidden_blocks, k, 0, keepdims=False)
            own_hidden = own_hidden[:, lo:hi, :].reshape(n_expert * count, hidden_dev)
            term = lax.dot_general(
                own_hidden, rows, (((0,), (0,)), ((), ())), preferred_element_type=jnp.float32
            )
            copy_acc = term if copy_acc is None else copy_acc + term

        gather_rows(rows_part, take, me, n_data)
    grad_hidden = grad_blocks.reshape(rows_all, hidden_dev)
    col_parts = [copy_acc.astype(jnp.bfloat16)]
    grad_cache, scores = finish(grad_hidden, parts)
    copy_grad = jnp.concatenate(col_parts, axis=1)
    share = hidden_dev // n_expert
    blocks = copy_grad.reshape(n_expert, share, width)
    gathered = lax.all_to_all(blocks, "expert", split_axis=0, concat_axis=0, tiled=True)
    same_expert = (copy_expert[:, None] == copy_expert[None, :]).astype(jnp.bfloat16)
    summed = jnp.dot(
        same_expert, gathered.reshape(n_expert, share * width), preferred_element_type=jnp.float32
    ).astype(jnp.bfloat16).reshape(n_expert, share, width)
    partial_scores = scores.reshape(n_data, places)
    row_scores = jnp.sum(
        lax.all_to_all(partial_scores, "dp", split_axis=0, concat_axis=0, tiled=True), axis=0
    ).reshape(n_expert, slots)
    high = row_scores.astype(jnp.bfloat16)
    rest = row_scores - high.astype(jnp.float32)
    mid = rest.astype(jnp.bfloat16)
    low = (rest - mid.astype(jnp.float32)).astype(jnp.bfloat16)
    extra = 128
    first = jnp.concatenate(
        [high, mid, low, jnp.zeros((n_expert, extra - 3 * slots), jnp.bfloat16)], axis=1
    )
    tail = jnp.concatenate(
        [first[:, None, :], jnp.zeros((n_expert, share - 1, extra), jnp.bfloat16)], axis=1
    )
    outbound = jnp.concatenate([summed, tail], axis=2)
    inbound = lax.all_to_all(outbound, "expert", split_axis=0, concat_axis=0, tiled=True)
    grad_weight = inbound[:, :, :width].reshape(1, hidden_dev, width)
    terms = inbound[:, 0, width : width + 3 * slots].astype(jnp.float32)
    score_back = (
        terms[:, :slots] + terms[:, slots : 2 * slots] + terms[:, 2 * slots :]
    ).reshape(places)
    assigned_score = jnp.dot(
        placing.astype(jnp.float32).T, score_back, precision=lax.Precision.HIGHEST
    )
    grad_probs = (assigned_score / gate_probs.reshape(-1).astype(jnp.float32)).reshape(
        gate_probs.shape
    )
    return (grad_cache[None], grad_weight, grad_probs)


def solution(mesh):
    placed = (
        P(("dp", "expert"), None),
        P(("dp", "expert"), None),
        P(("dp", "expert"), None),
        P(),
        P("expert", "dp", None),
        P("expert", None, None, "dp"),
    )
    return jax.shard_map(
        on_device,
        mesh=mesh,
        in_specs=placed,
        out_specs=(
            P("expert", None, None, "dp"),
            P("expert", "dp", None),
            P(("dp", "expert"), None),
        ),
        check_vma=False,
    )
```

```python
import jax
import jax.numpy as jnp
from jax import lax
from jax.sharding import PartitionSpec as P

def activations(cache):
    gate_pre = cache[0].astype(jnp.float32)
    up_pre = cache[1].astype(jnp.float32)
    sigmoid_gate = jax.nn.sigmoid(gate_pre)
    silu_gate = gate_pre * sigmoid_gate
    hidden = (silu_gate * up_pre).astype(jnp.bfloat16)
    return (hidden, gate_pre, up_pre, sigmoid_gate, silu_gate)


def finish(grad_hidden, parts):
    hidden, gate_pre, up_pre, sigmoid_gate, silu_gate = parts
    scores = jnp.sum(hidden.astype(jnp.float32) * grad_hidden, axis=1)
    grad_gate = grad_hidden * up_pre * sigmoid_gate * (1.0 + gate_pre * (1.0 - sigmoid_gate))
    grad_up = grad_hidden * silu_gate
    grad_cache = jnp.stack([grad_gate, grad_up]).astype(jnp.bfloat16)
    return (grad_cache, scores)


def placement(flat_ids, slots, places):
    count_all = flat_ids.shape[0]
    row_index = lax.broadcasted_iota(jnp.int32, (count_all, count_all), 0)
    col_index = lax.broadcasted_iota(jnp.int32, (count_all, count_all), 1)
    before = jnp.logical_and(flat_ids[:, None] == flat_ids[None, :], col_index < row_index)
    slot_rank = jnp.sum(before.astype(jnp.int32), axis=1)
    target = flat_ids * slots + slot_rank
    return lax.broadcasted_iota(jnp.int32, (places, count_all), 0) == target[None, :]


def gather_rows(rows_part, take, me, n_data):
    take(me, rows_part)
    if n_data == 8:
        chips = n_data // 2
        y = me // 2
        core = me % 2
        swap = [(j, j ^ 1) for j in range(n_data)]
        shift = [(2 * t, 2 * ((t + 1) % chips)) for t in range(chips)] + [
            (2 * t + 1, 2 * ((t - 1) % chips) + 1) for t in range(chips)
        ]
        partner = lax.ppermute(rows_part, "dp", swap)
        take(me ^ 1, partner)
        near_own = lax.ppermute(rows_part, "dp", shift)
        near_partner = lax.ppermute(partner, "dp", shift)
        src_near = jnp.where(core == 0, 2 * ((y - 1) % chips), 2 * ((y + 1) % chips) + 1)
        take(src_near, near_own)
        take(src_near ^ 1, near_partner)
        side_own = lax.ppermute(near_own, "dp", swap)
        side_partner = lax.ppermute(near_partner, "dp", swap)
        src_side = jnp.where(core == 0, 2 * ((y + 1) % chips) + 1, 2 * ((y - 1) % chips))
        take(src_side, side_own)
        take(src_side ^ 1, side_partner)
        far = lax.ppermute(near_own, "dp", shift)
        src_far = jnp.where(core == 0, 2 * ((y - 2) % chips), 2 * ((y + 2) % chips) + 1)
        take(src_far, far)
        far_side = lax.ppermute(far, "dp", swap)
        take(src_far ^ 1, far_side)
    else:
        forward = [(j, (j + 1) % n_data) for j in range(n_data)]
        ahead = rows_part
        for step in range(1, n_data):
            ahead = lax.ppermute(ahead, "dp", forward)
            take((me - step) % n_data, ahead)


def on_device(out_grad, gate_probs, copy_ids, copy_expert, w_down, swiglu_in):
    n_data = lax.axis_size("dp")
    n_expert = lax.axis_size("expert")
    cache = swiglu_in[0]
    weight = w_down[0]
    rows_all = cache.shape[1]
    hidden_dev = cache.shape[2]
    slots = rows_all // (n_data * n_expert)
    places = n_expert * slots
    width = out_grad.shape[1]
    tok_dev = out_grad.shape[0]
    top_count = copy_ids.shape[1]
    pair_count = tok_dev * top_count
    weighted = gate_probs.astype(jnp.float32)[:, :, None] * out_grad.astype(jnp.float32)[:, None, :]
    weighted = weighted.reshape(pair_count, width).astype(jnp.bfloat16)
    placing = placement(copy_ids.reshape(pair_count), slots, places)
    outgoing = jnp.dot(
        placing.astype(jnp.bfloat16), weighted, preferred_element_type=jnp.float32
    ).astype(jnp.bfloat16)
    outgoing = outgoing.reshape(n_expert, slots, width)
    parts = activations(cache)
    hidden = parts[0]
    me = lax.axis_index("dp")
    hidden_blocks = hidden.reshape(n_data, n_expert, slots, hidden_dev)
    copy_acc = None
    bounds = [(0, slots - 1), (slots - 1, slots)] if slots > 1 else [(0, slots)]
    grad_parts = []
    for lo, hi in bounds:
        count = hi - lo
        lanes = 128 if (count * width) % 128 == 0 else width
        send = outgoing[:, lo:hi, :].reshape(n_expert, count * width // lanes, lanes)
        arrived = lax.all_to_all(send, "expert", split_axis=0, concat_axis=0, tiled=True)
        rows_part = arrived.reshape(n_expert * count, width)
        hidden_part = hidden_blocks[:, :, lo:hi, :].reshape(n_data, n_expert * count, hidden_dev)
        grad_part = [jnp.zeros((n_data, n_expert * count, hidden_dev), jnp.float32)]

        def take(k, rows, hidden_part=hidden_part, grad_part=grad_part):
            nonlocal copy_acc
            part = lax.dot_general(
                rows, weight, (((1,), (1,)), ((), ())), preferred_element_type=jnp.float32
            )
            grad_part[0] = lax.dynamic_update_index_in_dim(grad_part[0], part, k, 0)
            own_hidden = lax.dynamic_index_in_dim(hidden_part, k, 0, keepdims=False)
            term = lax.dot_general(
                own_hidden, rows, (((0,), (0,)), ((), ())), preferred_element_type=jnp.float32
            )
            copy_acc = term if copy_acc is None else copy_acc + term

        gather_rows(rows_part, take, me, n_data)
        grad_parts.append(grad_part[0].reshape(n_data, n_expert, count, hidden_dev))
    grad_blocks = jnp.concatenate(grad_parts, axis=2)
    grad_hidden = grad_blocks.reshape(rows_all, hidden_dev)
    col_parts = [copy_acc.astype(jnp.bfloat16)]
    grad_cache, scores = finish(grad_hidden, parts)
    copy_grad = jnp.concatenate(col_parts, axis=1)
    share = hidden_dev // n_expert
    blocks = copy_grad.reshape(n_expert, share, width)
    gathered = lax.all_to_all(blocks, "expert", split_axis=0, concat_axis=0, tiled=True)
    same_expert = (copy_expert[:, None] == copy_expert[None, :]).astype(jnp.bfloat16)
    summed = jnp.dot(
        same_expert, gathered.reshape(n_expert, share * width), preferred_element_type=jnp.float32
    ).astype(jnp.bfloat16).reshape(n_expert, share, width)
    partial_scores = scores.reshape(n_data, places)
    row_scores = jnp.sum(
        lax.all_to_all(partial_scores, "dp", split_axis=0, concat_axis=0, tiled=True), axis=0
    ).reshape(n_expert, slots)
    high = row_scores.astype(jnp.bfloat16)
    rest = row_scores - high.astype(jnp.float32)
    mid = rest.astype(jnp.bfloat16)
    low = (rest - mid.astype(jnp.float32)).astype(jnp.bfloat16)
    extra = 128
    first = jnp.concatenate(
        [high, mid, low, jnp.zeros((n_expert, extra - 3 * slots), jnp.bfloat16)], axis=1
    )
    tail = jnp.concatenate(
        [first[:, None, :], jnp.zeros((n_expert, share - 1, extra), jnp.bfloat16)], axis=1
    )
    outbound = jnp.concatenate([summed, tail], axis=2)
    inbound = lax.all_to_all(outbound, "expert", split_axis=0, concat_axis=0, tiled=True)
    grad_weight = inbound[:, :, :width].reshape(1, hidden_dev, width)
    terms = inbound[:, 0, width : width + 3 * slots].astype(jnp.float32)
    score_back = (
        terms[:, :slots] + terms[:, slots : 2 * slots] + terms[:, 2 * slots :]
    ).reshape(places)
    assigned_score = jnp.dot(
        placing.astype(jnp.float32).T, score_back, precision=lax.Precision.HIGHEST
    )
    grad_probs = (assigned_score / gate_probs.reshape(-1).astype(jnp.float32)).reshape(
        gate_probs.shape
    )
    return (grad_cache[None], grad_weight, grad_probs)


def solution(mesh):
    placed = (
        P(("dp", "expert"), None),
        P(("dp", "expert"), None),
        P(("dp", "expert"), None),
        P(),
        P("expert", "dp", None),
        P("expert", None, None, "dp"),
    )
    return jax.shard_map(
        on_device,
        mesh=mesh,
        in_specs=placed,
        out_specs=(
            P("expert", None, None, "dp"),
            P("expert", "dp", None),
            P(("dp", "expert"), None),
        ),
        check_vma=False,
    )
```

```python
import jax
import jax.numpy as jnp
from jax import lax
from jax.sharding import PartitionSpec as P

def activations(cache):
    gate_pre = cache[0].astype(jnp.float32)
    up_pre = cache[1].astype(jnp.float32)
    sigmoid_gate = jax.nn.sigmoid(gate_pre)
    silu_gate = gate_pre * sigmoid_gate
    hidden = (silu_gate * up_pre).astype(jnp.bfloat16)
    return (hidden, gate_pre, up_pre, sigmoid_gate, silu_gate)


def finish(grad_hidden, parts):
    hidden, gate_pre, up_pre, sigmoid_gate, silu_gate = parts
    scores = jnp.sum(hidden.astype(jnp.float32) * grad_hidden, axis=1)
    grad_gate = grad_hidden * up_pre * sigmoid_gate * (1.0 + gate_pre * (1.0 - sigmoid_gate))
    grad_up = grad_hidden * silu_gate
    grad_cache = jnp.stack([grad_gate, grad_up]).astype(jnp.bfloat16)
    return (grad_cache, scores)


def placement(flat_ids, slots, places):
    count_all = flat_ids.shape[0]
    row_index = lax.broadcasted_iota(jnp.int32, (count_all, count_all), 0)
    col_index = lax.broadcasted_iota(jnp.int32, (count_all, count_all), 1)
    before = jnp.logical_and(flat_ids[:, None] == flat_ids[None, :], col_index < row_index)
    slot_rank = jnp.sum(before.astype(jnp.int32), axis=1)
    target = flat_ids * slots + slot_rank
    return lax.broadcasted_iota(jnp.int32, (places, count_all), 0) == target[None, :]


def on_device(out_grad, gate_probs, copy_ids, copy_expert, w_down, swiglu_in):
    n_data = lax.axis_size("dp")
    n_expert = lax.axis_size("expert")
    cache = swiglu_in[0]
    weight = w_down[0]
    rows_all = cache.shape[1]
    hidden_dev = cache.shape[2]
    slots = rows_all // (n_data * n_expert)
    places = n_expert * slots
    width = out_grad.shape[1]
    tok_dev = out_grad.shape[0]
    top_count = copy_ids.shape[1]
    pair_count = tok_dev * top_count
    weighted = gate_probs.astype(jnp.float32)[:, :, None] * out_grad.astype(jnp.float32)[:, None, :]
    weighted = weighted.reshape(pair_count, width).astype(jnp.bfloat16)
    placing = placement(copy_ids.reshape(pair_count), slots, places)
    outgoing = jnp.dot(
        placing.astype(jnp.bfloat16), weighted, preferred_element_type=jnp.float32
    ).astype(jnp.bfloat16)
    outgoing = outgoing.reshape(n_expert, slots, width)
    parts = activations(cache)
    hidden = parts[0]
    lanes = 128 if (slots * width) % 128 == 0 else width
    send = outgoing.reshape(n_expert, slots * width // lanes, lanes)
    arrived = lax.all_to_all(send, "expert", split_axis=0, concat_axis=0, tiled=True)
    rows_part = arrived.reshape(places, width)
    me = lax.axis_index("dp")
    hidden_blocks = hidden.reshape(n_data, places, hidden_dev)
    grad_blocks = jnp.zeros((n_data, places, hidden_dev), jnp.float32)
    copy_acc = None

    arrivals = []

    def take(k, rows):
        nonlocal copy_acc
        arrivals.append((k, rows))
        own_hidden = lax.dynamic_index_in_dim(hidden_blocks, k, 0, keepdims=False)
        term = lax.dot_general(
            own_hidden, rows, (((0,), (0,)), ((), ())), preferred_element_type=jnp.float32
        )
        copy_acc = term if copy_acc is None else copy_acc + term

    take(me, rows_part)
    if n_data == 8:
        chips = n_data // 2
        y = me // 2
        core = me % 2
        swap = [(j, j ^ 1) for j in range(n_data)]
        shift = [(2 * t, 2 * ((t + 1) % chips)) for t in range(chips)] + [
            (2 * t + 1, 2 * ((t - 1) % chips) + 1) for t in range(chips)
        ]
        partner = lax.ppermute(rows_part, "dp", swap)
        take(me ^ 1, partner)
        near_own = lax.ppermute(rows_part, "dp", shift)
        near_partner = lax.ppermute(partner, "dp", shift)
        src_near = jnp.where(core == 0, 2 * ((y - 1) % chips), 2 * ((y + 1) % chips) + 1)
        take(src_near, near_own)
        take(src_near ^ 1, near_partner)
        side_own = lax.ppermute(near_own, "dp", swap)
        side_partner = lax.ppermute(near_partner, "dp", swap)
        src_side = jnp.where(core == 0, 2 * ((y + 1) % chips) + 1, 2 * ((y - 1) % chips))
        take(src_side, side_own)
        take(src_side ^ 1, side_partner)
        far = lax.ppermute(near_own, "dp", shift)
        src_far = jnp.where(core == 0, 2 * ((y - 2) % chips), 2 * ((y + 2) % chips) + 1)
        take(src_far, far)
        far_side = lax.ppermute(far, "dp", swap)
        take(src_far ^ 1, far_side)
    else:
        forward = [(j, (j + 1) % n_data) for j in range(n_data)]
        ahead = rows_part
        for step in range(1, n_data):
            ahead = lax.ppermute(ahead, "dp", forward)
            take((me - step) % n_data, ahead)
    copy_grad, arrivals = lax.optimization_barrier((copy_acc.astype(jnp.bfloat16), arrivals))
    for k, rows in arrivals:
        part = lax.dot_general(
            rows, weight, (((1,), (1,)), ((), ())), preferred_element_type=jnp.float32
        )
        grad_blocks = lax.dynamic_update_index_in_dim(grad_blocks, part, k, 0)
    grad_hidden = grad_blocks.reshape(rows_all, hidden_dev)
    grad_cache, scores = finish(grad_hidden, parts)
    share = hidden_dev // n_expert
    blocks = copy_grad.reshape(n_expert, share, width)
    gathered = lax.all_to_all(blocks, "expert", split_axis=0, concat_axis=0, tiled=True)
    same_expert = (copy_expert[:, None] == copy_expert[None, :]).astype(jnp.bfloat16)
    summed = jnp.dot(
        same_expert, gathered.reshape(n_expert, share * width), preferred_element_type=jnp.float32
    ).astype(jnp.bfloat16).reshape(n_expert, share, width)
    partial_scores = scores.reshape(n_data, places)
    row_scores = lax.dynamic_index_in_dim(partial_scores, me, 0, keepdims=False)
    for step in range(1, n_data):
        outgoing_block = lax.dynamic_index_in_dim(
            partial_scores, (me + step) % n_data, 0, keepdims=False
        )
        row_scores = row_scores + lax.ppermute(
            outgoing_block, "dp", [(j, (j + step) % n_data) for j in range(n_data)]
        )
    row_scores = row_scores.reshape(n_expert, slots)
    high = row_scores.astype(jnp.bfloat16)
    rest = row_scores - high.astype(jnp.float32)
    mid = rest.astype(jnp.bfloat16)
    low = (rest - mid.astype(jnp.float32)).astype(jnp.bfloat16)
    extra = 128
    first = jnp.concatenate(
        [high, mid, low, jnp.zeros((n_expert, extra - 3 * slots), jnp.bfloat16)], axis=1
    )
    tail = jnp.concatenate(
        [first[:, None, :], jnp.zeros((n_expert, share - 1, extra), jnp.bfloat16)], axis=1
    )
    outbound = jnp.concatenate([summed, tail], axis=2)
    inbound = lax.all_to_all(outbound, "expert", split_axis=0, concat_axis=0, tiled=True)
    grad_weight = inbound[:, :, :width].reshape(1, hidden_dev, width)
    terms = inbound[:, 0, width : width + 3 * slots].astype(jnp.float32)
    score_back = (
        terms[:, :slots] + terms[:, slots : 2 * slots] + terms[:, 2 * slots :]
    ).reshape(places)
    assigned_score = jnp.dot(
        placing.astype(jnp.float32).T, score_back, precision=lax.Precision.HIGHEST
    )
    grad_probs = (assigned_score / gate_probs.reshape(-1).astype(jnp.float32)).reshape(
        gate_probs.shape
    )
    return (grad_cache[None], grad_weight, grad_probs)


def solution(mesh):
    placed = (
        P(("dp", "expert"), None),
        P(("dp", "expert"), None),
        P(("dp", "expert"), None),
        P(),
        P("expert", "dp", None),
        P("expert", None, None, "dp"),
    )
    return jax.shard_map(
        on_device,
        mesh=mesh,
        in_specs=placed,
        out_specs=(
            P("expert", None, None, "dp"),
            P("expert", "dp", None),
            P(("dp", "expert"), None),
        ),
        check_vma=False,
    )
```

```python
import jax
import jax.numpy as jnp
from jax import lax
from jax.sharding import PartitionSpec as P

def activations(cache):
    gate_pre = cache[0].astype(jnp.float32)
    up_pre = cache[1].astype(jnp.float32)
    sigmoid_gate = jax.nn.sigmoid(gate_pre)
    silu_gate = gate_pre * sigmoid_gate
    hidden = (silu_gate * up_pre).astype(jnp.bfloat16)
    return (hidden, gate_pre, up_pre, sigmoid_gate, silu_gate)


def finish(grad_hidden, parts):
    hidden, gate_pre, up_pre, sigmoid_gate, silu_gate = parts
    scores = jnp.sum(hidden.astype(jnp.float32) * grad_hidden, axis=1)
    grad_gate = grad_hidden * up_pre * sigmoid_gate * (1.0 + gate_pre * (1.0 - sigmoid_gate))
    grad_up = grad_hidden * silu_gate
    grad_cache = jnp.stack([grad_gate, grad_up]).astype(jnp.bfloat16)
    return (grad_cache, scores)


def placement(flat_ids, slots, places):
    count_all = flat_ids.shape[0]
    row_index = lax.broadcasted_iota(jnp.int32, (count_all, count_all), 0)
    col_index = lax.broadcasted_iota(jnp.int32, (count_all, count_all), 1)
    before = jnp.logical_and(flat_ids[:, None] == flat_ids[None, :], col_index < row_index)
    slot_rank = jnp.sum(before.astype(jnp.int32), axis=1)
    target = flat_ids * slots + slot_rank
    return lax.broadcasted_iota(jnp.int32, (places, count_all), 0) == target[None, :]


def on_device(out_grad, gate_probs, copy_ids, copy_expert, w_down, swiglu_in):
    n_data = lax.axis_size("dp")
    n_expert = lax.axis_size("expert")
    cache = swiglu_in[0]
    weight = w_down[0]
    rows_all = cache.shape[1]
    hidden_dev = cache.shape[2]
    slots = rows_all // (n_data * n_expert)
    places = n_expert * slots
    width = out_grad.shape[1]
    tok_dev = out_grad.shape[0]
    top_count = copy_ids.shape[1]
    pair_count = tok_dev * top_count
    weighted = gate_probs.astype(jnp.float32)[:, :, None] * out_grad.astype(jnp.float32)[:, None, :]
    weighted = weighted.reshape(pair_count, width).astype(jnp.bfloat16)
    placing = placement(copy_ids.reshape(pair_count), slots, places)
    outgoing = jnp.dot(
        placing.astype(jnp.bfloat16), weighted, preferred_element_type=jnp.float32
    ).astype(jnp.bfloat16)
    outgoing = outgoing.reshape(n_expert, slots, width)
    parts = activations(cache)
    hidden = parts[0]
    lanes = 128 if (slots * width) % 128 == 0 else width
    send = outgoing.reshape(n_expert, slots * width // lanes, lanes)
    arrived = lax.all_to_all(send, "expert", split_axis=0, concat_axis=0, tiled=True)
    rows_part = arrived.reshape(places, width)
    me = lax.axis_index("dp")
    hidden_blocks = hidden.reshape(n_data, places, hidden_dev)
    grad_blocks = jnp.zeros((n_data, places, hidden_dev), jnp.float32)
    copy_acc = None

    arrivals = []

    def take(k, rows):
        nonlocal copy_acc
        arrivals.append((k, rows))
        own_hidden = lax.dynamic_index_in_dim(hidden_blocks, k, 0, keepdims=False)
        term = lax.dot_general(
            own_hidden, rows, (((0,), (0,)), ((), ())), preferred_element_type=jnp.float32
        )
        copy_acc = term if copy_acc is None else copy_acc + term

    take(me, rows_part)
    if n_data == 8:
        chips = n_data // 2
        y = me // 2
        core = me % 2
        swap = [(j, j ^ 1) for j in range(n_data)]
        shift = [(2 * t, 2 * ((t + 1) % chips)) for t in range(chips)] + [
            (2 * t + 1, 2 * ((t - 1) % chips) + 1) for t in range(chips)
        ]
        partner = lax.ppermute(rows_part, "dp", swap)
        take(me ^ 1, partner)
        near_own = lax.ppermute(rows_part, "dp", shift)
        near_partner = lax.ppermute(partner, "dp", shift)
        src_near = jnp.where(core == 0, 2 * ((y - 1) % chips), 2 * ((y + 1) % chips) + 1)
        take(src_near, near_own)
        take(src_near ^ 1, near_partner)
        side_own = lax.ppermute(near_own, "dp", swap)
        side_partner = lax.ppermute(near_partner, "dp", swap)
        src_side = jnp.where(core == 0, 2 * ((y + 1) % chips) + 1, 2 * ((y - 1) % chips))
        take(src_side, side_own)
        take(src_side ^ 1, side_partner)
        far = lax.ppermute(near_own, "dp", shift)
        src_far = jnp.where(core == 0, 2 * ((y - 2) % chips), 2 * ((y + 2) % chips) + 1)
        take(src_far, far)
        far_side = lax.ppermute(far, "dp", swap)
        take(src_far ^ 1, far_side)
    else:
        forward = [(j, (j + 1) % n_data) for j in range(n_data)]
        ahead = rows_part
        for step in range(1, n_data):
            ahead = lax.ppermute(ahead, "dp", forward)
            take((me - step) % n_data, ahead)
    copy_grad, arrivals = lax.optimization_barrier((copy_acc.astype(jnp.bfloat16), arrivals))
    for k, rows in arrivals:
        part = lax.dot_general(
            rows, weight, (((1,), (1,)), ((), ())), preferred_element_type=jnp.float32
        )
        grad_blocks = lax.dynamic_update_index_in_dim(grad_blocks, part, k, 0)
    grad_hidden = grad_blocks.reshape(rows_all, hidden_dev)
    grad_cache, scores = finish(grad_hidden, parts)
    share = hidden_dev // n_expert
    blocks = copy_grad.reshape(n_expert, share, width)
    gathered = lax.all_to_all(blocks, "expert", split_axis=0, concat_axis=0, tiled=True)
    same_expert = (copy_expert[:, None] == copy_expert[None, :]).astype(jnp.bfloat16)
    summed = jnp.einsum(
        "ab,bqf->aqf", same_expert, gathered, preferred_element_type=jnp.float32
    ).astype(jnp.bfloat16)
    partial_scores = scores.reshape(n_data, places)
    row_scores = lax.dynamic_index_in_dim(partial_scores, me, 0, keepdims=False)
    for step in range(1, n_data):
        outgoing_block = lax.dynamic_index_in_dim(
            partial_scores, (me + step) % n_data, 0, keepdims=False
        )
        row_scores = row_scores + lax.ppermute(
            outgoing_block, "dp", [(j, (j + step) % n_data) for j in range(n_data)]
        )
    row_scores = row_scores.reshape(n_expert, slots)
    high = row_scores.astype(jnp.bfloat16)
    rest = row_scores - high.astype(jnp.float32)
    mid = rest.astype(jnp.bfloat16)
    low = (rest - mid.astype(jnp.float32)).astype(jnp.bfloat16)
    extra = 128
    first = jnp.concatenate(
        [high, mid, low, jnp.zeros((n_expert, extra - 3 * slots), jnp.bfloat16)], axis=1
    )
    tail = jnp.concatenate(
        [first[:, None, :], jnp.zeros((n_expert, share - 1, extra), jnp.bfloat16)], axis=1
    )
    holder = jnp.concatenate([jnp.zeros((n_expert, share, width), jnp.bfloat16), tail], axis=2)
    outbound = lax.dynamic_update_slice(holder, summed, (0, 0, 0))
    inbound = lax.all_to_all(outbound, "expert", split_axis=0, concat_axis=0, tiled=True)
    grad_weight = inbound[:, :, :width].reshape(1, hidden_dev, width)
    terms = inbound[:, 0, width : width + 3 * slots].astype(jnp.float32)
    score_back = (
        terms[:, :slots] + terms[:, slots : 2 * slots] + terms[:, 2 * slots :]
    ).reshape(places)
    assigned_score = jnp.dot(
        placing.astype(jnp.float32).T, score_back, precision=lax.Precision.HIGHEST
    )
    grad_probs = (assigned_score / gate_probs.reshape(-1).astype(jnp.float32)).reshape(
        gate_probs.shape
    )
    return (grad_cache[None], grad_weight, grad_probs)


def solution(mesh):
    placed = (
        P(("dp", "expert"), None),
        P(("dp", "expert"), None),
        P(("dp", "expert"), None),
        P(),
        P("expert", "dp", None),
        P("expert", None, None, "dp"),
    )
    return jax.shard_map(
        on_device,
        mesh=mesh,
        in_specs=placed,
        out_specs=(
            P("expert", None, None, "dp"),
            P("expert", "dp", None),
            P(("dp", "expert"), None),
        ),
        check_vma=False,
    )
```

```python
import jax
import jax.numpy as jnp
from jax import lax
from jax.sharding import PartitionSpec as P

def activations(cache):
    gate_pre = cache[0].astype(jnp.float32)
    up_pre = cache[1].astype(jnp.float32)
    sigmoid_gate = jax.nn.sigmoid(gate_pre)
    silu_gate = gate_pre * sigmoid_gate
    hidden = (silu_gate * up_pre).astype(jnp.bfloat16)
    return (hidden, gate_pre, up_pre, sigmoid_gate, silu_gate)


def finish(grad_hidden, parts):
    hidden, gate_pre, up_pre, sigmoid_gate, silu_gate = parts
    scores = jnp.sum(hidden.astype(jnp.float32) * grad_hidden, axis=1)
    grad_gate = grad_hidden * up_pre * sigmoid_gate * (1.0 + gate_pre * (1.0 - sigmoid_gate))
    grad_up = grad_hidden * silu_gate
    grad_cache = jnp.stack([grad_gate, grad_up]).astype(jnp.bfloat16)
    return (grad_cache, scores)


def placement(flat_ids, slots, places):
    count_all = flat_ids.shape[0]
    row_index = lax.broadcasted_iota(jnp.int32, (count_all, count_all), 0)
    col_index = lax.broadcasted_iota(jnp.int32, (count_all, count_all), 1)
    before = jnp.logical_and(flat_ids[:, None] == flat_ids[None, :], col_index < row_index)
    slot_rank = jnp.sum(before.astype(jnp.int32), axis=1)
    target = flat_ids * slots + slot_rank
    return lax.broadcasted_iota(jnp.int32, (places, count_all), 0) == target[None, :]


def on_device(out_grad, gate_probs, copy_ids, copy_expert, w_down, swiglu_in):
    n_data = lax.axis_size("dp")
    n_expert = lax.axis_size("expert")
    cache = swiglu_in[0]
    weight = w_down[0]
    rows_all = cache.shape[1]
    hidden_dev = cache.shape[2]
    slots = rows_all // (n_data * n_expert)
    places = n_expert * slots
    width = out_grad.shape[1]
    tok_dev = out_grad.shape[0]
    top_count = copy_ids.shape[1]
    pair_count = tok_dev * top_count
    weighted = gate_probs.astype(jnp.float32)[:, :, None] * out_grad.astype(jnp.float32)[:, None, :]
    weighted = weighted.reshape(pair_count, width).astype(jnp.bfloat16)
    placing = placement(copy_ids.reshape(pair_count), slots, places)
    outgoing = jnp.dot(
        placing.astype(jnp.bfloat16), weighted, preferred_element_type=jnp.float32
    ).astype(jnp.bfloat16)
    outgoing = outgoing.reshape(n_expert, slots, width)
    parts = activations(cache)
    hidden = parts[0]
    lanes = 128 if (slots * width) % 128 == 0 else width
    send = outgoing.reshape(n_expert, slots * width // lanes, lanes)
    arrived = lax.all_to_all(send, "expert", split_axis=0, concat_axis=0, tiled=True)
    rows_part = arrived.reshape(places, width)
    me = lax.axis_index("dp")
    hidden_blocks = hidden.reshape(n_data, places, hidden_dev)
    grad_blocks = jnp.zeros((n_data, places, hidden_dev), jnp.float32)
    copy_acc = None

    arrivals = []

    def take(k, rows):
        nonlocal copy_acc
        arrivals.append((k, rows))
        own_hidden = lax.dynamic_index_in_dim(hidden_blocks, k, 0, keepdims=False)
        term = lax.dot_general(
            own_hidden, rows, (((0,), (0,)), ((), ())), preferred_element_type=jnp.float32
        )
        copy_acc = term if copy_acc is None else copy_acc + term

    take(me, rows_part)
    if n_data == 8:
        chips = n_data // 2
        y = me // 2
        core = me % 2
        swap = [(j, j ^ 1) for j in range(n_data)]
        shift = [(2 * t, 2 * ((t + 1) % chips)) for t in range(chips)] + [
            (2 * t + 1, 2 * ((t - 1) % chips) + 1) for t in range(chips)
        ]
        diagonal = [(2 * t + 1, 2 * ((t + 1) % chips)) for t in range(chips)] + [
            (2 * t, 2 * ((t - 1) % chips) + 1) for t in range(chips)
        ]
        partner = lax.ppermute(rows_part, "dp", swap)
        take(me ^ 1, partner)
        near_own = lax.ppermute(rows_part, "dp", shift)
        near_partner = lax.ppermute(rows_part, "dp", diagonal)
        src_near = jnp.where(core == 0, 2 * ((y - 1) % chips), 2 * ((y + 1) % chips) + 1)
        take(src_near, near_own)
        take(src_near ^ 1, near_partner)
        side_own = lax.ppermute(near_own, "dp", swap)
        side_partner = lax.ppermute(near_partner, "dp", swap)
        src_side = jnp.where(core == 0, 2 * ((y + 1) % chips) + 1, 2 * ((y - 1) % chips))
        take(src_side, side_own)
        take(src_side ^ 1, side_partner)
        far = lax.ppermute(near_own, "dp", shift)
        src_far = jnp.where(core == 0, 2 * ((y - 2) % chips), 2 * ((y + 2) % chips) + 1)
        take(src_far, far)
        far_side = lax.ppermute(far, "dp", swap)
        take(src_far ^ 1, far_side)
    else:
        forward = [(j, (j + 1) % n_data) for j in range(n_data)]
        ahead = rows_part
        for step in range(1, n_data):
            ahead = lax.ppermute(ahead, "dp", forward)
            take((me - step) % n_data, ahead)
    copy_grad, arrivals = lax.optimization_barrier((copy_acc.astype(jnp.bfloat16), arrivals))
    for k, rows in arrivals:
        part = lax.dot_general(
            rows, weight, (((1,), (1,)), ((), ())), preferred_element_type=jnp.float32
        )
        grad_blocks = lax.dynamic_update_index_in_dim(grad_blocks, part, k, 0)
    grad_hidden = grad_blocks.reshape(rows_all, hidden_dev)
    grad_cache, scores = finish(grad_hidden, parts)
    share = hidden_dev // n_expert
    blocks = copy_grad.reshape(n_expert, share, width)
    gathered = lax.all_to_all(blocks, "expert", split_axis=0, concat_axis=0, tiled=True)
    same_expert = (copy_expert[:, None] == copy_expert[None, :]).astype(jnp.bfloat16)
    summed = jnp.einsum(
        "ab,bqf->aqf", same_expert, gathered, preferred_element_type=jnp.float32
    ).astype(jnp.bfloat16)
    partial_scores = scores.reshape(n_data, places)
    row_scores = lax.dynamic_index_in_dim(partial_scores, me, 0, keepdims=False)
    for step in range(1, n_data):
        outgoing_block = lax.dynamic_index_in_dim(
            partial_scores, (me + step) % n_data, 0, keepdims=False
        )
        row_scores = row_scores + lax.ppermute(
            outgoing_block, "dp", [(j, (j + step) % n_data) for j in range(n_data)]
        )
    row_scores = row_scores.reshape(n_expert, slots)
    high = row_scores.astype(jnp.bfloat16)
    rest = row_scores - high.astype(jnp.float32)
    mid = rest.astype(jnp.bfloat16)
    low = (rest - mid.astype(jnp.float32)).astype(jnp.bfloat16)
    extra = 128
    first = jnp.concatenate(
        [high, mid, low, jnp.zeros((n_expert, extra - 3 * slots), jnp.bfloat16)], axis=1
    )
    tail = jnp.concatenate(
        [first[:, None, :], jnp.zeros((n_expert, share - 1, extra), jnp.bfloat16)], axis=1
    )
    holder = jnp.concatenate([jnp.zeros((n_expert, share, width), jnp.bfloat16), tail], axis=2)
    outbound = lax.dynamic_update_slice(holder, summed, (0, 0, 0))
    inbound = lax.all_to_all(outbound, "expert", split_axis=0, concat_axis=0, tiled=True)
    grad_weight = inbound[:, :, :width].reshape(1, hidden_dev, width)
    terms = inbound[:, 0, width : width + 3 * slots].astype(jnp.float32)
    score_back = (
        terms[:, :slots] + terms[:, slots : 2 * slots] + terms[:, 2 * slots :]
    ).reshape(places)
    assigned_score = jnp.dot(
        placing.astype(jnp.float32).T, score_back, precision=lax.Precision.HIGHEST
    )
    grad_probs = (assigned_score / gate_probs.reshape(-1).astype(jnp.float32)).reshape(
        gate_probs.shape
    )
    return (grad_cache[None], grad_weight, grad_probs)


def solution(mesh):
    placed = (
        P(("dp", "expert"), None),
        P(("dp", "expert"), None),
        P(("dp", "expert"), None),
        P(),
        P("expert", "dp", None),
        P("expert", None, None, "dp"),
    )
    return jax.shard_map(
        on_device,
        mesh=mesh,
        in_specs=placed,
        out_specs=(
            P("expert", None, None, "dp"),
            P("expert", "dp", None),
            P(("dp", "expert"), None),
        ),
        check_vma=False,
    )
```

```python
import jax
import jax.numpy as jnp
from jax import lax
from jax.sharding import PartitionSpec as P

def activations(cache):
    gate_pre = cache[0].astype(jnp.float32)
    up_pre = cache[1].astype(jnp.float32)
    sigmoid_gate = jax.nn.sigmoid(gate_pre)
    silu_gate = gate_pre * sigmoid_gate
    hidden = (silu_gate * up_pre).astype(jnp.bfloat16)
    return (hidden, gate_pre, up_pre, sigmoid_gate, silu_gate)


def finish(grad_hidden, parts):
    hidden, gate_pre, up_pre, sigmoid_gate, silu_gate = parts
    scores = jnp.sum(hidden.astype(jnp.float32) * grad_hidden, axis=1)
    grad_gate = grad_hidden * up_pre * sigmoid_gate * (1.0 + gate_pre * (1.0 - sigmoid_gate))
    grad_up = grad_hidden * silu_gate
    grad_cache = jnp.stack([grad_gate, grad_up]).astype(jnp.bfloat16)
    return (grad_cache, scores)


def placement(flat_ids, slots, places):
    count_all = flat_ids.shape[0]
    row_index = lax.broadcasted_iota(jnp.int32, (count_all, count_all), 0)
    col_index = lax.broadcasted_iota(jnp.int32, (count_all, count_all), 1)
    before = jnp.logical_and(flat_ids[:, None] == flat_ids[None, :], col_index < row_index)
    slot_rank = jnp.sum(before.astype(jnp.int32), axis=1)
    target = flat_ids * slots + slot_rank
    return lax.broadcasted_iota(jnp.int32, (places, count_all), 0) == target[None, :]


def on_device(out_grad, gate_probs, copy_ids, copy_expert, w_down, swiglu_in):
    n_data = lax.axis_size("dp")
    n_expert = lax.axis_size("expert")
    cache = swiglu_in[0]
    weight = w_down[0]
    rows_all = cache.shape[1]
    hidden_dev = cache.shape[2]
    slots = rows_all // (n_data * n_expert)
    places = n_expert * slots
    width = out_grad.shape[1]
    tok_dev = out_grad.shape[0]
    top_count = copy_ids.shape[1]
    pair_count = tok_dev * top_count
    weighted = gate_probs.astype(jnp.float32)[:, :, None] * out_grad.astype(jnp.float32)[:, None, :]
    weighted = weighted.reshape(pair_count, width).astype(jnp.bfloat16)
    placing = placement(copy_ids.reshape(pair_count), slots, places)
    outgoing = jnp.dot(
        placing.astype(jnp.bfloat16), weighted, preferred_element_type=jnp.float32
    ).astype(jnp.bfloat16)
    outgoing = outgoing.reshape(n_expert, slots, width)
    parts = activations(cache)
    hidden = parts[0]
    lanes = 128 if (slots * width) % 128 == 0 else width
    send = outgoing.reshape(n_expert, slots * width // lanes, lanes)
    arrived = lax.all_to_all(send, "expert", split_axis=0, concat_axis=0, tiled=True)
    rows_part = arrived.reshape(places, width)
    me = lax.axis_index("dp")
    share = hidden_dev // n_expert
    hidden_blocks = hidden.reshape(n_data, places, hidden_dev)
    grad_blocks = jnp.zeros((n_data, places, hidden_dev), jnp.float32)
    copy_acc = None

    arrivals = []

    def take(k, rows):
        nonlocal copy_acc
        arrivals.append((k, rows))
        own_hidden = lax.dynamic_index_in_dim(hidden_blocks, k, 0, keepdims=False)
        term = jnp.einsum(
            "rbq,rf->bqf",
            own_hidden.reshape(own_hidden.shape[0], n_expert, share),
            rows,
            preferred_element_type=jnp.float32,
        )
        copy_acc = term if copy_acc is None else copy_acc + term

    take(me, rows_part)
    if n_data == 8:
        chips = n_data // 2
        y = me // 2
        core = me % 2
        swap = [(j, j ^ 1) for j in range(n_data)]
        shift = [(2 * t, 2 * ((t + 1) % chips)) for t in range(chips)] + [
            (2 * t + 1, 2 * ((t - 1) % chips) + 1) for t in range(chips)
        ]
        diagonal = [(2 * t + 1, 2 * ((t + 1) % chips)) for t in range(chips)] + [
            (2 * t, 2 * ((t - 1) % chips) + 1) for t in range(chips)
        ]
        partner = lax.ppermute(rows_part, "dp", swap)
        take(me ^ 1, partner)
        near_own = lax.ppermute(rows_part, "dp", shift)
        near_partner = lax.ppermute(rows_part, "dp", diagonal)
        src_near = jnp.where(core == 0, 2 * ((y - 1) % chips), 2 * ((y + 1) % chips) + 1)
        take(src_near, near_own)
        take(src_near ^ 1, near_partner)
        side_own = lax.ppermute(near_own, "dp", swap)
        side_partner = lax.ppermute(near_partner, "dp", swap)
        src_side = jnp.where(core == 0, 2 * ((y + 1) % chips) + 1, 2 * ((y - 1) % chips))
        take(src_side, side_own)
        take(src_side ^ 1, side_partner)
        far = lax.ppermute(near_own, "dp", shift)
        src_far = jnp.where(core == 0, 2 * ((y - 2) % chips), 2 * ((y + 2) % chips) + 1)
        take(src_far, far)
        far_side = lax.ppermute(far, "dp", swap)
        take(src_far ^ 1, far_side)
    else:
        forward = [(j, (j + 1) % n_data) for j in range(n_data)]
        ahead = rows_part
        for step in range(1, n_data):
            ahead = lax.ppermute(ahead, "dp", forward)
            take((me - step) % n_data, ahead)
    copy_grad, arrivals = lax.optimization_barrier((copy_acc.astype(jnp.bfloat16), arrivals))
    for k, rows in arrivals:
        part = lax.dot_general(
            rows, weight, (((1,), (1,)), ((), ())), preferred_element_type=jnp.float32
        )
        grad_blocks = lax.dynamic_update_index_in_dim(grad_blocks, part, k, 0)
    grad_hidden = grad_blocks.reshape(rows_all, hidden_dev)
    grad_cache, scores = finish(grad_hidden, parts)
    blocks = copy_grad
    gathered = lax.all_to_all(blocks, "expert", split_axis=0, concat_axis=0, tiled=True)
    same_expert = (copy_expert[:, None] == copy_expert[None, :]).astype(jnp.bfloat16)
    summed = jnp.einsum(
        "ab,bqf->aqf", same_expert, gathered, preferred_element_type=jnp.float32
    ).astype(jnp.bfloat16)
    partial_scores = scores.reshape(n_data, places)
    row_scores = lax.dynamic_index_in_dim(partial_scores, me, 0, keepdims=False)
    for step in range(1, n_data):
        outgoing_block = lax.dynamic_index_in_dim(
            partial_scores, (me + step) % n_data, 0, keepdims=False
        )
        row_scores = row_scores + lax.ppermute(
            outgoing_block, "dp", [(j, (j + step) % n_data) for j in range(n_data)]
        )
    row_scores = row_scores.reshape(n_expert, slots)
    high = row_scores.astype(jnp.bfloat16)
    rest = row_scores - high.astype(jnp.float32)
    mid = rest.astype(jnp.bfloat16)
    low = (rest - mid.astype(jnp.float32)).astype(jnp.bfloat16)
    extra = 128
    first = jnp.concatenate(
        [high, mid, low, jnp.zeros((n_expert, extra - 3 * slots), jnp.bfloat16)], axis=1
    )
    tail = jnp.concatenate(
        [first[:, None, :], jnp.zeros((n_expert, share - 1, extra), jnp.bfloat16)], axis=1
    )
    holder = jnp.concatenate([jnp.zeros((n_expert, share, width), jnp.bfloat16), tail], axis=2)
    outbound = lax.dynamic_update_slice(holder, summed, (0, 0, 0))
    inbound = lax.all_to_all(outbound, "expert", split_axis=0, concat_axis=0, tiled=True)
    grad_weight = inbound[:, :, :width].reshape(1, hidden_dev, width)
    terms = inbound[:, 0, width : width + 3 * slots].astype(jnp.float32)
    score_back = (
        terms[:, :slots] + terms[:, slots : 2 * slots] + terms[:, 2 * slots :]
    ).reshape(places)
    assigned_score = jnp.dot(
        placing.astype(jnp.float32).T, score_back, precision=lax.Precision.HIGHEST
    )
    grad_probs = (assigned_score / gate_probs.reshape(-1).astype(jnp.float32)).reshape(
        gate_probs.shape
    )
    return (grad_cache[None], grad_weight, grad_probs)


def solution(mesh):
    placed = (
        P(("dp", "expert"), None),
        P(("dp", "expert"), None),
        P(("dp", "expert"), None),
        P(),
        P("expert", "dp", None),
        P("expert", None, None, "dp"),
    )
    return jax.shard_map(
        on_device,
        mesh=mesh,
        in_specs=placed,
        out_specs=(
            P("expert", None, None, "dp"),
            P("expert", "dp", None),
            P(("dp", "expert"), None),
        ),
        check_vma=False,
    )
```

```python
import jax
import jax.numpy as jnp
from jax import lax
from jax.sharding import PartitionSpec as P

def activations(cache):
    gate_pre = cache[0].astype(jnp.float32)
    up_pre = cache[1].astype(jnp.float32)
    sigmoid_gate = jax.nn.sigmoid(gate_pre)
    silu_gate = gate_pre * sigmoid_gate
    hidden = (silu_gate * up_pre).astype(jnp.bfloat16)
    return (hidden, gate_pre, up_pre, sigmoid_gate, silu_gate)


def finish(grad_hidden, parts):
    hidden, gate_pre, up_pre, sigmoid_gate, silu_gate = parts
    scores = jnp.sum(hidden.astype(jnp.float32) * grad_hidden, axis=1)
    grad_gate = grad_hidden * up_pre * sigmoid_gate * (1.0 + gate_pre * (1.0 - sigmoid_gate))
    grad_up = grad_hidden * silu_gate
    grad_cache = jnp.stack([grad_gate, grad_up]).astype(jnp.bfloat16)
    return (grad_cache, scores)


def placement(flat_ids, slots, places):
    count_all = flat_ids.shape[0]
    row_index = lax.broadcasted_iota(jnp.int32, (count_all, count_all), 0)
    col_index = lax.broadcasted_iota(jnp.int32, (count_all, count_all), 1)
    before = jnp.logical_and(flat_ids[:, None] == flat_ids[None, :], col_index < row_index)
    slot_rank = jnp.sum(before.astype(jnp.int32), axis=1)
    target = flat_ids * slots + slot_rank
    return lax.broadcasted_iota(jnp.int32, (places, count_all), 0) == target[None, :]


def on_device(out_grad, gate_probs, copy_ids, copy_expert, w_down, swiglu_in):
    n_data = lax.axis_size("dp")
    n_expert = lax.axis_size("expert")
    cache = swiglu_in[0]
    weight = w_down[0]
    rows_all = cache.shape[1]
    hidden_dev = cache.shape[2]
    slots = rows_all // (n_data * n_expert)
    places = n_expert * slots
    width = out_grad.shape[1]
    tok_dev = out_grad.shape[0]
    top_count = copy_ids.shape[1]
    pair_count = tok_dev * top_count
    weighted = gate_probs.astype(jnp.float32)[:, :, None] * out_grad.astype(jnp.float32)[:, None, :]
    weighted = weighted.reshape(pair_count, width).astype(jnp.bfloat16)
    placing = placement(copy_ids.reshape(pair_count), slots, places)
    outgoing = jnp.dot(
        placing.astype(jnp.bfloat16), weighted, preferred_element_type=jnp.float32
    ).astype(jnp.bfloat16)
    outgoing = outgoing.reshape(n_expert, slots, width)
    parts = activations(cache)
    hidden = parts[0]
    lanes = 128 if (slots * width) % 128 == 0 else width
    send = outgoing.reshape(n_expert, slots * width // lanes, lanes)
    arrived = lax.all_to_all(send, "expert", split_axis=0, concat_axis=0, tiled=True)
    rows_part = arrived.reshape(places, width)
    me = lax.axis_index("dp")
    share = hidden_dev // n_expert
    hidden_blocks = hidden.reshape(n_data, places, hidden_dev)
    grad_blocks = jnp.zeros((n_data, places, hidden_dev), jnp.float32)
    copy_acc = None

    arrivals = []

    def take(k, rows):
        nonlocal copy_acc
        arrivals.append((k, rows))
        own_hidden = lax.dynamic_index_in_dim(hidden_blocks, k, 0, keepdims=False)
        term = jnp.einsum(
            "rbq,rf->bqf",
            own_hidden.reshape(own_hidden.shape[0], n_expert, share),
            rows,
            preferred_element_type=jnp.float32,
        )
        copy_acc = term if copy_acc is None else copy_acc + term

    take(me, rows_part)
    if n_data == 8:
        chips = n_data // 2
        y = me // 2
        core = me % 2
        swap = [(j, j ^ 1) for j in range(n_data)]
        shift = [(2 * t, 2 * ((t + 1) % chips)) for t in range(chips)] + [
            (2 * t + 1, 2 * ((t - 1) % chips) + 1) for t in range(chips)
        ]
        diagonal = [(2 * t + 1, 2 * ((t + 1) % chips)) for t in range(chips)] + [
            (2 * t, 2 * ((t - 1) % chips) + 1) for t in range(chips)
        ]
        partner = lax.ppermute(rows_part, "dp", swap)
        take(me ^ 1, partner)
        near_own = lax.ppermute(rows_part, "dp", shift)
        near_partner = lax.ppermute(rows_part, "dp", diagonal)
        src_near = jnp.where(core == 0, 2 * ((y - 1) % chips), 2 * ((y + 1) % chips) + 1)
        take(src_near, near_own)
        take(src_near ^ 1, near_partner)
        side_own = lax.ppermute(near_own, "dp", swap)
        side_partner = lax.ppermute(near_partner, "dp", swap)
        src_side = jnp.where(core == 0, 2 * ((y + 1) % chips) + 1, 2 * ((y - 1) % chips))
        take(src_side, side_own)
        take(src_side ^ 1, side_partner)
        reach = [(2 * t, 2 * ((t + 2) % chips)) for t in range(chips)] + [
            (2 * t + 1, 2 * ((t - 2) % chips) + 1) for t in range(chips)
        ]
        far = lax.ppermute(rows_part, "dp", reach)
        src_far = jnp.where(core == 0, 2 * ((y - 2) % chips), 2 * ((y + 2) % chips) + 1)
        take(src_far, far)
        far_side = lax.ppermute(far, "dp", swap)
        take(src_far ^ 1, far_side)
    else:
        forward = [(j, (j + 1) % n_data) for j in range(n_data)]
        ahead = rows_part
        for step in range(1, n_data):
            ahead = lax.ppermute(ahead, "dp", forward)
            take((me - step) % n_data, ahead)
    copy_grad, arrivals = lax.optimization_barrier((copy_acc.astype(jnp.bfloat16), arrivals))
    for k, rows in arrivals:
        part = lax.dot_general(
            rows, weight, (((1,), (1,)), ((), ())), preferred_element_type=jnp.float32
        )
        grad_blocks = lax.dynamic_update_index_in_dim(grad_blocks, part, k, 0)
    grad_hidden = grad_blocks.reshape(rows_all, hidden_dev)
    grad_cache, scores = finish(grad_hidden, parts)
    blocks = copy_grad
    gathered = lax.all_to_all(blocks, "expert", split_axis=0, concat_axis=0, tiled=True)
    same_expert = (copy_expert[:, None] == copy_expert[None, :]).astype(jnp.bfloat16)
    summed = jnp.einsum(
        "ab,bqf->aqf", same_expert, gathered, preferred_element_type=jnp.float32
    ).astype(jnp.bfloat16)
    partial_scores = scores.reshape(n_data, places)
    row_scores = lax.dynamic_index_in_dim(partial_scores, me, 0, keepdims=False)
    for step in range(1, n_data):
        outgoing_block = lax.dynamic_index_in_dim(
            partial_scores, (me + step) % n_data, 0, keepdims=False
        )
        row_scores = row_scores + lax.ppermute(
            outgoing_block, "dp", [(j, (j + step) % n_data) for j in range(n_data)]
        )
    row_scores = row_scores.reshape(n_expert, slots)
    high = row_scores.astype(jnp.bfloat16)
    rest = row_scores - high.astype(jnp.float32)
    mid = rest.astype(jnp.bfloat16)
    low = (rest - mid.astype(jnp.float32)).astype(jnp.bfloat16)
    extra = 128
    first = jnp.concatenate(
        [high, mid, low, jnp.zeros((n_expert, extra - 3 * slots), jnp.bfloat16)], axis=1
    )
    tail = jnp.concatenate(
        [first[:, None, :], jnp.zeros((n_expert, share - 1, extra), jnp.bfloat16)], axis=1
    )
    holder = jnp.concatenate([jnp.zeros((n_expert, share, width), jnp.bfloat16), tail], axis=2)
    outbound = lax.dynamic_update_slice(holder, summed, (0, 0, 0))
    inbound = lax.all_to_all(outbound, "expert", split_axis=0, concat_axis=0, tiled=True)
    grad_weight = inbound[:, :, :width].reshape(1, hidden_dev, width)
    terms = inbound[:, 0, width : width + 3 * slots].astype(jnp.float32)
    score_back = (
        terms[:, :slots] + terms[:, slots : 2 * slots] + terms[:, 2 * slots :]
    ).reshape(places)
    assigned_score = jnp.dot(
        placing.astype(jnp.float32).T, score_back, precision=lax.Precision.HIGHEST
    )
    grad_probs = (assigned_score / gate_probs.reshape(-1).astype(jnp.float32)).reshape(
        gate_probs.shape
    )
    return (grad_cache[None], grad_weight, grad_probs)


def solution(mesh):
    placed = (
        P(("dp", "expert"), None),
        P(("dp", "expert"), None),
        P(("dp", "expert"), None),
        P(),
        P("expert", "dp", None),
        P("expert", None, None, "dp"),
    )
    return jax.shard_map(
        on_device,
        mesh=mesh,
        in_specs=placed,
        out_specs=(
            P("expert", None, None, "dp"),
            P("expert", "dp", None),
            P(("dp", "expert"), None),
        ),
        check_vma=False,
    )
```
